32 devices in a mesh: seq: 8 (over y, x, core), head: 4 (over z).
Axes of the slice: x: 2, y: 2, z: 4, core: 2. Of those that a mesh axis runs over, the one named last changes fastest.
Arguments:
- queries: bfloat16 [4096, 4096], P('seq', 'head'), may hold values from -6 to 6
- keys: bfloat16 [4096, 4096], P('seq', 'head'), may hold values from -6 to 6
- values: bfloat16 [4096, 4096], P('seq', 'head'), may hold values from -48 to 48
- gate_logits: bfloat16 [4096, 4096], P('seq', 'head'), may hold values from -8 to 8
- out_weight: bfloat16 [4096, 6144], P('head'), may hold values from -0.125 to 0.125
Outputs:
- layer_out: bfloat16 [4096, 6144], P('seq', 'head')
The draws below stay inside these ranges and needn't reach their ends.
All inputs are finite; a program needn't handle non-finite values.
Results may differ from the reference program's by a relative error of at most 0.02.
Values may be sent and summed in bfloat16 or wider, within the bound.
No kernel may reach another device: no remote copies, remote signals or barrier semaphores. Data moves between devices by JAX's collectives and lax.ppermute only.
A program may use at most 64 MiB of HBM per device.

```python
import jax
import jax.numpy as jnp
from jax import lax

D = 6144
HEADS = 32
HEAD_DIM = 128
BLOCK = 512
TOKENS = 4096
HD = 4096
N_HEAD = 4


def draw_values(key, part):
    first_key, second_key = jax.random.split(key, 2)
    columns = HEADS * HEAD_DIM
    head_number = (jnp.arange(columns) // HEAD_DIM).astype(jnp.float32)
    ramp = 3.0 ** (head_number / max(HEADS - 1, 1))
    column_gain = jax.random.uniform(second_key, (columns,), jnp.float32, 0.6, 1.6)
    base = jnp.clip(jax.random.normal(first_key, (TOKENS, columns), jnp.float32), -6.0, 6.0)
    return (base * ramp[None, :] * column_gain[None, :]).astype(jnp.bfloat16)


def spiked(entries, stream_key, source, target, blocks, factor):
    def block_of(axis_at):
        return (jnp.arange(entries.shape[axis_at]) // (entries.shape[axis_at] // blocks)).reshape((-1,) + (1,) * (entries.ndim - 1 - axis_at))

    first = jax.random.permutation(stream_key, blocks)[block_of(target)]
    far = (block_of(target) + blocks // 2) % blocks
    return jnp.where((block_of(source) == first) | (block_of(source) == far), factor * entries, entries)


def steps_of(stream_key, extent, pieces, smallest, top_value):
    loudness = 1.0
    for dim, blocks in pieces:
        draws = jax.random.uniform(jax.random.fold_in(jax.random.fold_in(stream_key, 6), dim), (blocks,), jnp.float32, smallest / len(pieces), top_value / len(pieces))
        loudness = loudness * jnp.repeat(jnp.exp(draws), extent[dim] // blocks).reshape((-1,) + (1,) * (len(extent) - 1 - dim))
    return loudness


def centred(stream_key, shape, width, bound, shards=(), kind=jnp.bfloat16):
    values = jax.random.normal(stream_key, shape, jnp.float32) * width
    if len(shards) > 0:
        values = steps_of(stream_key, shape, shards, -0.22, 0.18) * values
    return jnp.clip(values, min=-bound, max=bound).astype(kind)


def noise_with(own_key, extent, deviation, reach, shards, heavy, held_as=jnp.bfloat16):
    array = deviation * jax.random.normal(own_key, extent, jnp.float32)
    if shards:
        array = array * steps_of(own_key, extent, shards, -0.22, 0.18)
    return jnp.clip(spiked(array, jax.random.fold_in(own_key, 3), *heavy), -reach, reach).astype(held_as)


def setup_inputs(seed: int = 0) -> dict:
    splits = jax.random.split(jax.random.key(seed), 6)
    queries = centred(splits[0], (TOKENS, HD), 1.0, 6.0, ((0, 8), (1, 4)))
    keys = centred(splits[1], (TOKENS, HD), 1.0, 6.0, ((0, 8), (1, 4)))
    values = draw_values(jax.random.fold_in(splits[5], 71), 0)
    gate_logits = centred(splits[3], (TOKENS, HD), 1.5, 8.0, ((0, 8), (1, 4)))
    out_weight = noise_with(splits[4], (HD, D), HD ** -0.5, 0.125, ((0, 4),), (0, 1, 4, 2.0))
    return dict(queries=queries, keys=keys, values=values, gate_logits=gate_logits, out_weight=out_weight)


def activate(raw_input):
    return jax.nn.silu(raw_input.astype(jnp.float32)).astype(jnp.bfloat16)

def reference(queries, keys, values, gate_logits, out_weight):
    block_count = TOKENS // BLOCK
    active_q = activate(queries).reshape(block_count, BLOCK, HEADS, HEAD_DIM)
    active_k = activate(keys).reshape(block_count, BLOCK, HEADS, HEAD_DIM)
    active_v = activate(values).reshape(block_count, BLOCK, HEADS, HEAD_DIM)
    causal_mask = jnp.tril(jnp.ones((BLOCK, BLOCK), jnp.float32))

    def advance(carried, blocks):
        query_blk, key_blk, value_blk = blocks
        query_f = query_blk.astype(jnp.float32)
        key_f = key_blk.astype(jnp.float32)
        value_f = value_blk.astype(jnp.float32)
        scores = (jnp.einsum('thd,shd->hts', query_f, key_f) * causal_mask).astype(jnp.bfloat16)
        within_block = jnp.einsum('hts,shd->thd', scores.astype(jnp.float32), value_f)
        state_bf = carried.astype(jnp.bfloat16).astype(jnp.float32)
        from_state = jnp.einsum('thd,hde->the', query_f, state_bf)
        updated = carried + jnp.einsum('shd,she->hde', key_f, value_f)
        return (updated, within_block + from_state)
    initial = jnp.zeros((HEADS, HEAD_DIM, HEAD_DIM), jnp.float32)
    final_state, attended = lax.scan(advance, initial, (active_q, active_k, active_v))
    attended = attended.reshape(TOKENS, HD)
    mean_square = lax.optimization_barrier(jnp.mean(attended * attended, axis=-1, keepdims=True))
    gate = jax.nn.sigmoid(gate_logits.astype(jnp.float32))
    normed = (attended * lax.rsqrt(mean_square + 1e-06) * gate).astype(jnp.bfloat16)
    group_width = HD // N_HEAD
    normed_groups = normed.reshape(TOKENS, N_HEAD, group_width).transpose(1, 0, 2)
    weight_groups = out_weight.reshape(N_HEAD, group_width, D)

    def accumulate(total, group):
        normed_part, weight_part = group
        partial_sum = jnp.dot(normed_part, weight_part, preferred_element_type=jnp.float32)
        return (total + partial_sum.astype(jnp.bfloat16).astype(jnp.float32), None)
    total, unused = lax.scan(accumulate, jnp.zeros((TOKENS, D), jnp.float32), (normed_groups, weight_groups))
    return total.astype(jnp.bfloat16)
```

```python
import jax
import jax.numpy as jnp
from jax import lax
from jax.sharding import PartitionSpec as P

HEADS = 32
HEAD_DIM = 128
OUT_CHUNKS = 4


def activate(raw_input):
    return jax.nn.silu(raw_input.astype(jnp.float32)).astype(jnp.bfloat16)


def exclusive_prefix(span_total, axis_name):
    count = lax.axis_size(axis_name)
    running = span_total
    earlier = jnp.zeros_like(span_total)
    shift = 1
    while shift < count:
        pairs = [(i, i + shift) for i in range(count - shift)]
        arrived = lax.ppermute(running.astype(jnp.bfloat16), axis_name, pairs).astype(jnp.float32)
        earlier = earlier + arrived
        running = running + arrived
        shift *= 2
    return earlier


def body(queries, keys, values, gate_logits, out_weight):
    tokens_here = queries.shape[0]
    feature_count = queries.shape[1]
    heads_here = feature_count // HEAD_DIM
    block_rows = min(512, tokens_here)
    block_count = tokens_here // block_rows
    shape_blocks = (block_count, block_rows, heads_here, HEAD_DIM)
    active_q = activate(queries).reshape(shape_blocks)
    active_k = activate(keys).reshape(shape_blocks)
    active_v = activate(values).reshape(shape_blocks)
    block_states = jnp.einsum(
        "nshd,nshe->nhde", active_k, active_v, preferred_element_type=jnp.float32
    )
    span_total = jnp.sum(block_states, axis=0)
    earlier_local = jnp.cumsum(block_states, axis=0) - block_states
    prefix = exclusive_prefix(span_total, "seq")
    before = (prefix[None] + earlier_local).astype(jnp.bfloat16)
    causal_mask = jnp.tril(jnp.ones((block_rows, block_rows), jnp.float32))
    scores = jnp.einsum("nthd,nshd->nhts", active_q, active_k, preferred_element_type=jnp.float32)
    scores = (scores * causal_mask).astype(jnp.bfloat16)
    within_block = jnp.einsum(
        "nhts,nshd->nthd", scores, active_v, preferred_element_type=jnp.float32
    )
    from_state = jnp.einsum("nthd,nhde->nthe", active_q, before, preferred_element_type=jnp.float32)
    attended = (within_block + from_state).reshape(tokens_here, feature_count)
    square_sums = jnp.sum(attended * attended, axis=-1)
    gate = jax.nn.sigmoid(gate_logits.astype(jnp.float32))
    gated = (attended * gate).astype(jnp.bfloat16)
    chunks = OUT_CHUNKS if tokens_here % (OUT_CHUNKS * 8) == 0 else 1
    chunk_rows = tokens_here // chunks
    pieces = []
    for c in range(chunks):
        part = gated[c * chunk_rows:(c + 1) * chunk_rows]
        product = lax.dot_general(
            out_weight, part, (((0,), (1,)), ((), ())), preferred_element_type=jnp.float32
        ).astype(jnp.bfloat16)
        pieces.append(lax.psum_scatter(product, "head", scatter_dimension=0, tiled=True))
    reduced = jnp.concatenate(pieces, axis=1).astype(jnp.float32)
    total_squares = lax.psum(square_sums, "head")
    scaling = lax.rsqrt(total_squares / (HEADS * HEAD_DIM) + 1e-06)
    return (reduced.T * scaling[:, None]).astype(jnp.bfloat16)


def solution(mesh):
    return jax.shard_map(
        body,
        mesh=mesh,
        in_specs=(
            P("seq", "head"),
            P("seq", "head"),
            P("seq", "head"),
            P("seq", "head"),
            P("head", None),
        ),
        out_specs=P("seq", "head"),
        check_vma=False,
    )
```

```python
import jax
import jax.numpy as jnp
from jax import lax
from jax.sharding import PartitionSpec as P

HEADS = 32
HEAD_DIM = 128
OUT_CHUNKS = 1


def activate(raw_input):
    return jax.nn.silu(raw_input.astype(jnp.float32)).astype(jnp.bfloat16)


def body(queries, keys, values, gate_logits, out_weight):
    tokens_here = queries.shape[0]
    feature_count = queries.shape[1]
    heads_here = feature_count // HEAD_DIM
    block_rows = min(512, tokens_here)
    block_count = tokens_here // block_rows
    shape_blocks = (block_count, block_rows, heads_here, HEAD_DIM)
    active_q = activate(queries).reshape(shape_blocks)
    active_k = activate(keys).reshape(shape_blocks)
    active_v = activate(values).reshape(shape_blocks)
    block_states = jnp.einsum(
        "nshd,nshe->nhde", active_k, active_v, preferred_element_type=jnp.float32
    )
    span_total = jnp.sum(block_states, axis=0)
    earlier_local = jnp.cumsum(block_states, axis=0) - block_states
    my_index = lax.axis_index("seq")
    shards = lax.all_gather(
        span_total[None].astype(jnp.bfloat16), "seq", axis=0, tiled=True
    ).astype(jnp.float32)
    positions = jnp.arange(shards.shape[0], dtype=jnp.int32)
    weights = (positions < my_index).astype(jnp.float32)
    prefix = jnp.sum(shards * weights[:, None, None, None], axis=0)
    causal_mask = jnp.tril(jnp.ones((block_rows, block_rows), jnp.float32))
    scores = jnp.einsum("nthd,nshd->nhts", active_q, active_k, preferred_element_type=jnp.float32)
    scores = (scores * causal_mask).astype(jnp.bfloat16)
    within_block = jnp.einsum(
        "nhts,nshd->nthd", scores, active_v, preferred_element_type=jnp.float32
    )
    within_block, prefix = lax.optimization_barrier((within_block, prefix))
    before = (prefix[None] + earlier_local).astype(jnp.bfloat16)
    from_state = jnp.einsum("nthd,nhde->nthe", active_q, before, preferred_element_type=jnp.float32)
    attended = (within_block + from_state).reshape(tokens_here, feature_count)
    square_sums = jnp.sum(attended * attended, axis=-1)
    gate = jax.nn.sigmoid(gate_logits.astype(jnp.float32))
    gated = (attended * gate).astype(jnp.bfloat16)
    chunks = OUT_CHUNKS if tokens_here % (OUT_CHUNKS * 8) == 0 else 1
    chunk_rows = tokens_here // chunks
    pieces = []
    for c in range(chunks):
        part = gated[c * chunk_rows:(c + 1) * chunk_rows]
        product = lax.dot_general(
            out_weight, part, (((0,), (1,)), ((), ())), preferred_element_type=jnp.float32
        ).astype(jnp.bfloat16)
        pieces.append(lax.psum_scatter(product, "head", scatter_dimension=0, tiled=True))
    reduced = jnp.concatenate(pieces, axis=1).astype(jnp.float32)
    total_squares = lax.psum(square_sums, "head")
    scaling = lax.rsqrt(total_squares / (HEADS * HEAD_DIM) + 1e-06)
    return (reduced.T * scaling[:, None]).astype(jnp.bfloat16)


def solution(mesh):
    return jax.shard_map(
        body,
        mesh=mesh,
        in_specs=(
            P("seq", "head"),
            P("seq", "head"),
            P("seq", "head"),
            P("seq", "head"),
            P("head", None),
        ),
        out_specs=P("seq", "head"),
        check_vma=False,
    )
```

```python
import jax
import jax.numpy as jnp
from jax import lax
from jax.sharding import PartitionSpec as P

HEADS = 32
HEAD_DIM = 128
OUT_CHUNKS = 1


def activate(raw_input):
    return jax.nn.silu(raw_input.astype(jnp.float32)).astype(jnp.bfloat16)


def body(queries, keys, values, gate_logits, out_weight):
    tokens_here = queries.shape[0]
    feature_count = queries.shape[1]
    heads_here = feature_count // HEAD_DIM
    block_rows = min(512, tokens_here)
    block_count = tokens_here // block_rows
    shape_blocks = (block_count, block_rows, heads_here, HEAD_DIM)
    active_q = activate(queries).reshape(shape_blocks)
    active_k = activate(keys).reshape(shape_blocks)
    active_v = activate(values).reshape(shape_blocks)
    block_states = jnp.einsum(
        "nshd,nshe->nhde", active_k, active_v, preferred_element_type=jnp.float32
    )
    span_total = jnp.sum(block_states, axis=0)
    earlier_local = jnp.cumsum(block_states, axis=0) - block_states
    partner = lax.ppermute(span_total.astype(jnp.bfloat16), "core", [(0, 1), (1, 0)])
    partner = partner.astype(jnp.float32)
    chip_total = span_total + partner
    chip_index = lax.axis_index("chip")
    core_index = lax.axis_index("core")
    shards = lax.all_gather(
        chip_total[None].astype(jnp.bfloat16), "chip", axis=0, tiled=True
    ).astype(jnp.float32)
    positions = jnp.arange(shards.shape[0], dtype=jnp.int32)
    weights = (positions < chip_index).astype(jnp.float32)
    prefix = jnp.sum(shards * weights[:, None, None, None], axis=0)
    prefix = prefix + partner * (core_index == 1).astype(jnp.float32)
    causal_mask = jnp.tril(jnp.ones((block_rows, block_rows), jnp.float32))
    scores = jnp.einsum("nthd,nshd->nhts", active_q, active_k, preferred_element_type=jnp.float32)
    scores = (scores * causal_mask).astype(jnp.bfloat16)
    within_block = jnp.einsum(
        "nhts,nshd->nthd", scores, active_v, preferred_element_type=jnp.float32
    )
    within_block, prefix = lax.optimization_barrier((within_block, prefix))
    before = (prefix[None] + earlier_local).astype(jnp.bfloat16)
    from_state = jnp.einsum("nthd,nhde->nthe", active_q, before, preferred_element_type=jnp.float32)
    attended = (within_block + from_state).reshape(tokens_here, feature_count)
    square_sums = jnp.sum(attended * attended, axis=-1)
    gate = jax.nn.sigmoid(gate_logits.astype(jnp.float32))
    gated = (attended * gate).astype(jnp.bfloat16)
    chunks = OUT_CHUNKS if tokens_here % (OUT_CHUNKS * 8) == 0 else 1
    chunk_rows = tokens_here // chunks
    pieces = []
    for c in range(chunks):
        part = gated[c * chunk_rows:(c + 1) * chunk_rows]
        product = lax.dot_general(
            out_weight, part, (((0,), (1,)), ((), ())), preferred_element_type=jnp.float32
        ).astype(jnp.bfloat16)
        pieces.append(lax.psum_scatter(product, "head", scatter_dimension=0, tiled=True))
    reduced = jnp.concatenate(pieces, axis=1).astype(jnp.float32)
    total_squares = lax.psum(square_sums, "head")
    scaling = lax.rsqrt(total_squares / (HEADS * HEAD_DIM) + 1e-06)
    return (reduced.T * scaling[:, None]).astype(jnp.bfloat16)


def solution(mesh):
    seq_size = mesh.shape["seq"]
    head_size = mesh.shape["head"]
    split = jax.sharding.Mesh(
        mesh.devices.reshape(seq_size // 2, 2, head_size), ("chip", "core", "head")
    )
    rows = ("chip", "core")
    return jax.shard_map(
        body,
        mesh=split,
        in_specs=(
            P(rows, "head"),
            P(rows, "head"),
            P(rows, "head"),
            P(rows, "head"),
            P("head", None),
        ),
        out_specs=P(rows, "head"),
        check_vma=False,
    )
```

```python
import jax
import jax.numpy as jnp
from jax import lax
from jax.sharding import PartitionSpec as P

HEADS = 32
HEAD_DIM = 128
OUT_CHUNKS = 1


def activate(raw_input):
    return jax.nn.silu(raw_input.astype(jnp.float32)).astype(jnp.bfloat16)


def exclusive_prefix(span_total, axis_name):
    count = lax.axis_size(axis_name)
    my_index = lax.axis_index(axis_name)
    if count & (count - 1):
        shards = lax.all_gather(
            span_total[None].astype(jnp.bfloat16), axis_name, axis=0, tiled=True
        ).astype(jnp.float32)
        positions = jnp.arange(count, dtype=jnp.int32)
        weights = (positions < my_index).astype(jnp.float32)
        return jnp.sum(shards * weights[:, None, None, None], axis=0)
    group_total = span_total
    prefix = jnp.zeros_like(span_total)
    bit = 1
    while bit < count:
        pairs = [(i, i ^ bit) for i in range(count)]
        arrived = lax.ppermute(group_total.astype(jnp.bfloat16), axis_name, pairs)
        arrived = arrived.astype(jnp.float32)
        upper = ((my_index // bit) % 2).astype(jnp.float32)
        prefix = prefix + upper * arrived
        group_total = group_total + arrived
        bit *= 2
    return prefix


def body(queries, keys, values, gate_logits, out_weight):
    tokens_here = queries.shape[0]
    feature_count = queries.shape[1]
    heads_here = feature_count // HEAD_DIM
    block_rows = min(512, tokens_here)
    block_count = tokens_here // block_rows
    shape_blocks = (block_count, block_rows, heads_here, HEAD_DIM)
    active_q = activate(queries).reshape(shape_blocks)
    active_k = activate(keys).reshape(shape_blocks)
    active_v = activate(values).reshape(shape_blocks)
    block_states = jnp.einsum(
        "nshd,nshe->nhde", active_k, active_v, preferred_element_type=jnp.float32
    )
    span_total = jnp.sum(block_states, axis=0)
    earlier_local = jnp.cumsum(block_states, axis=0) - block_states
    prefix = exclusive_prefix(span_total, "seq")
    causal_mask = jnp.tril(jnp.ones((block_rows, block_rows), jnp.float32))
    scores = jnp.einsum("nthd,nshd->nhts", active_q, active_k, preferred_element_type=jnp.float32)
    scores = (scores * causal_mask).astype(jnp.bfloat16)
    within_block = jnp.einsum(
        "nhts,nshd->nthd", scores, active_v, preferred_element_type=jnp.float32
    )
    within_block, prefix = lax.optimization_barrier((within_block, prefix))
    before = (prefix[None] + earlier_local).astype(jnp.bfloat16)
    from_state = jnp.einsum("nthd,nhde->nthe", active_q, before, preferred_element_type=jnp.float32)
    attended = (within_block + from_state).reshape(tokens_here, feature_count)
    square_sums = jnp.sum(attended * attended, axis=-1)
    gate = jax.nn.sigmoid(gate_logits.astype(jnp.float32))
    gated = (attended * gate).astype(jnp.bfloat16)
    chunks = OUT_CHUNKS if tokens_here % (OUT_CHUNKS * 8) == 0 else 1
    chunk_rows = tokens_here // chunks
    pieces = []
    for c in range(chunks):
        part = gated[c * chunk_rows:(c + 1) * chunk_rows]
        product = lax.dot_general(
            out_weight, part, (((0,), (1,)), ((), ())), preferred_element_type=jnp.float32
        ).astype(jnp.bfloat16)
        pieces.append(lax.psum_scatter(product, "head", scatter_dimension=0, tiled=True))
    reduced = jnp.concatenate(pieces, axis=1).astype(jnp.float32)
    total_squares = lax.psum(square_sums, "head")
    scaling = lax.rsqrt(total_squares / (HEADS * HEAD_DIM) + 1e-06)
    return (reduced.T * scaling[:, None]).astype(jnp.bfloat16)


def solution(mesh):
    return jax.shard_map(
        body,
        mesh=mesh,
        in_specs=(
            P("seq", "head"),
            P("seq", "head"),
            P("seq", "head"),
            P("seq", "head"),
            P("head", None),
        ),
        out_specs=P("seq", "head"),
        check_vma=False,
    )
```

```python
import jax
import jax.numpy as jnp
from jax import lax
from jax.sharding import PartitionSpec as P

HEADS = 32
HEAD_DIM = 128


def activate(raw_input):
    return jax.nn.silu(raw_input.astype(jnp.float32)).astype(jnp.bfloat16)


def exclusive_prefix(span_total, axis_name):
    count = lax.axis_size(axis_name)
    my_index = lax.axis_index(axis_name)
    if count & (count - 1):
        shards = lax.all_gather(
            span_total[None].astype(jnp.bfloat16), axis_name, axis=0, tiled=True
        ).astype(jnp.float32)
        positions = jnp.arange(count, dtype=jnp.int32)
        weights = (positions < my_index).astype(jnp.float32)
        return jnp.sum(shards * weights[:, None, None, None], axis=0)
    group_total = span_total
    prefix = jnp.zeros_like(span_total)
    bit = 1
    while bit < count:
        pairs = [(i, i ^ bit) for i in range(count)]
        arrived = lax.ppermute(group_total.astype(jnp.bfloat16), axis_name, pairs)
        arrived = arrived.astype(jnp.float32)
        upper = ((my_index // bit) % 2).astype(jnp.float32)
        prefix = prefix + upper * arrived
        group_total = group_total + arrived
        bit *= 2
    return prefix


def shard_product(gated, out_weight, shard, width):
    columns = lax.dynamic_slice_in_dim(out_weight, shard * width, width, axis=1)
    return jnp.dot(gated, columns, preferred_element_type=jnp.float32)


def line_reduce_scatter(gated, out_weight, axis_name):
    count = lax.axis_size(axis_name)
    here = lax.axis_index(axis_name)
    width = out_weight.shape[1] // count
    from_left = None
    from_right = None
    for step in range(1, count):
        right_shard = jnp.clip(here + count - step, 0, count - 1)
        left_shard = jnp.clip(here - count + step, 0, count - 1)
        to_right = shard_product(gated, out_weight, right_shard, width)
        to_left = shard_product(gated, out_weight, left_shard, width)
        to_right, to_left = lax.optimization_barrier((to_right, to_left))
        if from_left is not None:
            to_right = to_right + from_left
            to_left = to_left + from_right
        right_pairs = [(i, i + 1) for i in range(step) if i + 1 < count]
        left_pairs = [(i, i - 1) for i in range(count - step, count) if i >= 1]
        from_left = lax.ppermute(to_right.astype(jnp.bfloat16), axis_name, right_pairs)
        from_right = lax.ppermute(to_left.astype(jnp.bfloat16), axis_name, left_pairs)
        from_left = from_left.astype(jnp.float32)
        from_right = from_right.astype(jnp.float32)
    own = shard_product(gated, out_weight, here, width)
    if from_left is None:
        return own
    return own + from_left + from_right


def body(queries, keys, values, gate_logits, out_weight):
    tokens_here = queries.shape[0]
    feature_count = queries.shape[1]
    heads_here = feature_count // HEAD_DIM
    block_rows = min(512, tokens_here)
    block_count = tokens_here // block_rows
    shape_blocks = (block_count, block_rows, heads_here, HEAD_DIM)
    active_q = activate(queries).reshape(shape_blocks)
    active_k = activate(keys).reshape(shape_blocks)
    active_v = activate(values).reshape(shape_blocks)
    block_states = jnp.einsum(
        "nshd,nshe->nhde", active_k, active_v, preferred_element_type=jnp.float32
    )
    span_total = jnp.sum(block_states, axis=0)
    earlier_local = jnp.cumsum(block_states, axis=0) - block_states
    prefix = exclusive_prefix(span_total, "seq")
    causal_mask = jnp.tril(jnp.ones((block_rows, block_rows), jnp.float32))
    scores = jnp.einsum("nthd,nshd->nhts", active_q, active_k, preferred_element_type=jnp.float32)
    scores = (scores * causal_mask).astype(jnp.bfloat16)
    within_block = jnp.einsum(
        "nhts,nshd->nthd", scores, active_v, preferred_element_type=jnp.float32
    )
    within_block, prefix = lax.optimization_barrier((within_block, prefix))
    before = (prefix[None] + earlier_local).astype(jnp.bfloat16)
    from_state = jnp.einsum("nthd,nhde->nthe", active_q, before, preferred_element_type=jnp.float32)
    attended = (within_block + from_state).reshape(tokens_here, feature_count)
    square_sums = jnp.sum(attended * attended, axis=-1)
    gate = jax.nn.sigmoid(gate_logits.astype(jnp.float32))
    gated = (attended * gate).astype(jnp.bfloat16)
    total_squares = lax.psum(square_sums, "head")
    scaling = lax.rsqrt(total_squares / (HEADS * HEAD_DIM) + 1e-06)
    reduced = line_reduce_scatter(gated, out_weight, "head")
    return (reduced * scaling[:, None]).astype(jnp.bfloat16)


def solution(mesh):
    return jax.shard_map(
        body,
        mesh=mesh,
        in_specs=(
            P("seq", "head"),
            P("seq", "head"),
            P("seq", "head"),
            P("seq", "head"),
            P("head", None),
        ),
        out_specs=P("seq", "head"),
        check_vma=False,
    )
```

```python
import jax
import jax.numpy as jnp
from jax import lax
from jax.sharding import PartitionSpec as P

HEADS = 32
HEAD_DIM = 128


def activate(raw_input):
    return jax.nn.silu(raw_input.astype(jnp.float32)).astype(jnp.bfloat16)


def exclusive_prefix(span_total, axis_name):
    count = lax.axis_size(axis_name)
    my_index = lax.axis_index(axis_name)
    if count & (count - 1):
        shards = lax.all_gather(
            span_total[None].astype(jnp.bfloat16), axis_name, axis=0, tiled=True
        ).astype(jnp.float32)
        positions = jnp.arange(count, dtype=jnp.int32)
        weights = (positions < my_index).astype(jnp.float32)
        return jnp.sum(shards * weights[:, None, None, None], axis=0)
    group_total = span_total
    prefix = jnp.zeros_like(span_total)
    bit = 1
    while bit < count:
        pairs = [(i, i ^ bit) for i in range(count)]
        arrived = lax.ppermute(group_total.astype(jnp.bfloat16), axis_name, pairs)
        arrived = arrived.astype(jnp.float32)
        upper = ((my_index // bit) % 2).astype(jnp.float32)
        prefix = prefix + upper * arrived
        group_total = group_total + arrived
        bit *= 2
    return prefix


def shard_product(gated, out_weight, shard, width):
    columns = lax.dynamic_slice_in_dim(out_weight, shard * width, width, axis=1)
    return jnp.dot(gated, columns, preferred_element_type=jnp.float32)


def line_reduce_scatter(gated, out_weight, axis_name, square_sums):
    count = lax.axis_size(axis_name)
    here = lax.axis_index(axis_name)
    width = out_weight.shape[1] // count
    from_left = None
    from_right = None
    for step in range(1, count):
        right_shard = jnp.clip(here + count - step, 0, count - 1)
        left_shard = jnp.clip(here - count + step, 0, count - 1)
        if 2 * step <= count:
            shard = jnp.where(here < step, right_shard, left_shard)
            to_right = lax.optimization_barrier(shard_product(gated, out_weight, shard, width))
            to_left = to_right
        else:
            to_right = shard_product(gated, out_weight, right_shard, width)
            to_left = shard_product(gated, out_weight, left_shard, width)
            to_right, to_left = lax.optimization_barrier((to_right, to_left))
        if from_left is not None:
            to_right = to_right + from_left
            to_left = to_left + from_right
        right_pairs = [(i, i + 1) for i in range(step) if i + 1 < count]
        left_pairs = [(i, i - 1) for i in range(count - step, count) if i >= 1]
        from_left = lax.ppermute(to_right.astype(jnp.bfloat16), axis_name, right_pairs)
        from_right = lax.ppermute(to_left.astype(jnp.bfloat16), axis_name, left_pairs)
        from_left = from_left.astype(jnp.float32)
        from_right = from_right.astype(jnp.float32)
    own = shard_product(gated, out_weight, here, width)
    own, square_sums = lax.optimization_barrier((own, square_sums))
    total_squares = lax.psum(square_sums, axis_name)
    scaling = lax.rsqrt(total_squares / (HEADS * HEAD_DIM) + 1e-06)
    if from_left is not None:
        own = own + from_left + from_right
    return own * scaling[:, None]


def body(queries, keys, values, gate_logits, out_weight):
    tokens_here = queries.shape[0]
    feature_count = queries.shape[1]
    heads_here = feature_count // HEAD_DIM
    block_rows = min(512, tokens_here)
    block_count = tokens_here // block_rows
    shape_blocks = (block_count, block_rows, heads_here, HEAD_DIM)
    active_q = activate(queries).reshape(shape_blocks)
    active_k = activate(keys).reshape(shape_blocks)
    active_v = activate(values).reshape(shape_blocks)
    block_states = jnp.einsum(
        "nshd,nshe->nhde", active_k, active_v, preferred_element_type=jnp.float32
    )
    span_total = jnp.sum(block_states, axis=0)
    earlier_local = jnp.cumsum(block_states, axis=0) - block_states
    prefix = exclusive_prefix(span_total, "seq")
    causal_mask = jnp.tril(jnp.ones((block_rows, block_rows), jnp.float32))
    scores = jnp.einsum("nthd,nshd->nhts", active_q, active_k, preferred_element_type=jnp.float32)
    scores = (scores * causal_mask).astype(jnp.bfloat16)
    within_block = jnp.einsum(
        "nhts,nshd->nthd", scores, active_v, preferred_element_type=jnp.float32
    )
    within_block, prefix = lax.optimization_barrier((within_block, prefix))
    before = (prefix[None] + earlier_local).astype(jnp.bfloat16)
    from_state = jnp.einsum("nthd,nhde->nthe", active_q, before, preferred_element_type=jnp.float32)
    attended = (within_block + from_state).reshape(tokens_here, feature_count)
    square_sums = jnp.sum(attended * attended, axis=-1)
    gate = jax.nn.sigmoid(gate_logits.astype(jnp.float32))
    gated = (attended * gate).astype(jnp.bfloat16)
    reduced = line_reduce_scatter(gated, out_weight, "head", square_sums)
    return reduced.astype(jnp.bfloat16)


def solution(mesh):
    return jax.shard_map(
        body,
        mesh=mesh,
        in_specs=(
            P("seq", "head"),
            P("seq", "head"),
            P("seq", "head"),
            P("seq", "head"),
            P("head", None),
        ),
        out_specs=P("seq", "head"),
        check_vma=False,
    )
```

```python
import jax
import jax.numpy as jnp
from jax import lax
from jax.sharding import PartitionSpec as P

HEADS = 32
HEAD_DIM = 128


def activate(raw_input):
    return jax.nn.silu(raw_input.astype(jnp.float32)).astype(jnp.bfloat16)


def exclusive_prefix(span_total, axis_name):
    count = lax.axis_size(axis_name)
    my_index = lax.axis_index(axis_name)
    if count & (count - 1):
        shards = lax.all_gather(
            span_total[None].astype(jnp.bfloat16), axis_name, axis=0, tiled=True
        ).astype(jnp.float32)
        positions = jnp.arange(count, dtype=jnp.int32)
        weights = (positions < my_index).astype(jnp.float32)
        return jnp.sum(shards * weights[:, None, None, None], axis=0)
    group_total = span_total
    prefix = jnp.zeros_like(span_total)
    bit = 1
    while bit < count:
        pairs = [(i, i ^ bit) for i in range(count)]
        arrived = lax.ppermute(group_total.astype(jnp.bfloat16), axis_name, pairs)
        arrived = arrived.astype(jnp.float32)
        upper = ((my_index // bit) % 2).astype(jnp.float32)
        prefix = prefix + upper * arrived
        group_total = group_total + arrived
        bit *= 2
    return prefix


def shard_product(gated, out_weight, shard, width):
    columns = lax.dynamic_slice_in_dim(out_weight, shard * width, width, axis=1)
    return jnp.dot(gated, columns, preferred_element_type=jnp.float32)


def butterfly_sum(values, axis_name):
    count = lax.axis_size(axis_name)
    if count & (count - 1):
        return lax.psum(values, axis_name)
    bit = 1
    while bit < count:
        values = values + lax.ppermute(values, axis_name, [(i, i ^ bit) for i in range(count)])
        bit *= 2
    return values


def line_reduce_scatter(gated, out_weight, axis_name, total_squares):
    count = lax.axis_size(axis_name)
    here = lax.axis_index(axis_name)
    width = out_weight.shape[1] // count
    from_left = None
    from_right = None
    for step in range(1, count):
        right_shard = jnp.clip(here + count - step, 0, count - 1)
        left_shard = jnp.clip(here - count + step, 0, count - 1)
        if 2 * step <= count:
            shard = jnp.where(here < step, right_shard, left_shard)
            to_right = shard_product(gated, out_weight, shard, width)
            if step == min(2, count - 1):
                to_right, total_squares = lax.optimization_barrier((to_right, total_squares))
            else:
                to_right = lax.optimization_barrier(to_right)
            to_left = to_right
        else:
            to_right = shard_product(gated, out_weight, right_shard, width)
            to_left = shard_product(gated, out_weight, left_shard, width)
            if step == min(2, count - 1):
                to_right, to_left, total_squares = lax.optimization_barrier(
                    (to_right, to_left, total_squares)
                )
            else:
                to_right, to_left = lax.optimization_barrier((to_right, to_left))
        if from_left is not None:
            to_right = to_right + from_left
            to_left = to_left + from_right
        right_pairs = [(i, i + 1) for i in range(step) if i + 1 < count]
        left_pairs = [(i, i - 1) for i in range(count - step, count) if i >= 1]
        from_left = lax.ppermute(to_right.astype(jnp.bfloat16), axis_name, right_pairs)
        from_right = lax.ppermute(to_left.astype(jnp.bfloat16), axis_name, left_pairs)
        from_left = from_left.astype(jnp.float32)
        from_right = from_right.astype(jnp.float32)
    own = shard_product(gated, out_weight, here, width)
    scaling = lax.rsqrt(total_squares / (HEADS * HEAD_DIM) + 1e-06)
    if from_left is not None:
        own = own + from_left + from_right
    return own * scaling[:, None]


def body(queries, keys, values, gate_logits, out_weight):
    tokens_here = queries.shape[0]
    feature_count = queries.shape[1]
    heads_here = feature_count // HEAD_DIM
    block_rows = min(512, tokens_here)
    block_count = tokens_here // block_rows
    shape_blocks = (block_count, block_rows, heads_here, HEAD_DIM)
    active_q = activate(queries).reshape(shape_blocks)
    active_k = activate(keys).reshape(shape_blocks)
    active_v = activate(values).reshape(shape_blocks)
    block_states = jnp.einsum(
        "nshd,nshe->nhde", active_k, active_v, preferred_element_type=jnp.float32
    )
    span_total = jnp.sum(block_states, axis=0)
    earlier_local = jnp.cumsum(block_states, axis=0) - block_states
    prefix = exclusive_prefix(span_total, "seq")
    causal_mask = jnp.tril(jnp.ones((block_rows, block_rows), jnp.float32))
    scores = jnp.einsum("nthd,nshd->nhts", active_q, active_k, preferred_element_type=jnp.float32)
    scores = (scores * causal_mask).astype(jnp.bfloat16)
    within_block = jnp.einsum(
        "nhts,nshd->nthd", scores, active_v, preferred_element_type=jnp.float32
    )
    within_block, prefix = lax.optimization_barrier((within_block, prefix))
    before = (prefix[None] + earlier_local).astype(jnp.bfloat16)
    from_state = jnp.einsum("nthd,nhde->nthe", active_q, before, preferred_element_type=jnp.float32)
    attended = (within_block + from_state).reshape(tokens_here, feature_count)
    square_sums = jnp.sum(attended * attended, axis=-1)
    gate = jax.nn.sigmoid(gate_logits.astype(jnp.float32))
    gated = (attended * gate).astype(jnp.bfloat16)
    total_squares = butterfly_sum(square_sums, "head")
    reduced = line_reduce_scatter(gated, out_weight, "head", total_squares)
    return reduced.astype(jnp.bfloat16)


def solution(mesh):
    return jax.shard_map(
        body,
        mesh=mesh,
        in_specs=(
            P("seq", "head"),
            P("seq", "head"),
            P("seq", "head"),
            P("seq", "head"),
            P("head", None),
        ),
        out_specs=P("seq", "head"),
        check_vma=False,
    )
```

```python
import jax
import jax.numpy as jnp
from jax import lax
from jax.sharding import PartitionSpec as P

HEADS = 32
HEAD_DIM = 128


def activate(raw_input):
    return jax.nn.silu(raw_input.astype(jnp.float32)).astype(jnp.bfloat16)


def exclusive_prefix(span_total, axis_name):
    count = lax.axis_size(axis_name)
    my_index = lax.axis_index(axis_name)
    if count & (count - 1):
        shards = lax.all_gather(
            span_total[None].astype(jnp.bfloat16), axis_name, axis=0, tiled=True
        ).astype(jnp.float32)
        positions = jnp.arange(count, dtype=jnp.int32)
        weights = (positions < my_index).astype(jnp.float32)
        return jnp.sum(shards * weights[:, None, None, None], axis=0)
    group_total = span_total
    prefix = jnp.zeros_like(span_total)
    bit = 1
    while bit < count:
        pairs = [(i, i ^ bit) for i in range(count)]
        arrived = lax.ppermute(group_total.astype(jnp.bfloat16), axis_name, pairs)
        arrived = arrived.astype(jnp.float32)
        upper = ((my_index // bit) % 2).astype(jnp.float32)
        prefix = prefix + upper * arrived
        group_total = group_total + arrived
        bit *= 2
    return prefix


def shard_product(gated, out_weight, shard, width):
    columns = lax.dynamic_slice_in_dim(out_weight, shard * width, width, axis=1)
    return jnp.dot(gated, columns, preferred_element_type=jnp.float32)


def butterfly_sum(values, axis_name):
    count = lax.axis_size(axis_name)
    if count & (count - 1):
        return lax.psum(values, axis_name)
    bit = 1
    while bit < count:
        values = values + lax.ppermute(values, axis_name, [(i, i ^ bit) for i in range(count)])
        bit *= 2
    return values


def line_reduce_scatter(gated, out_weight, axis_name, total_squares):
    count = lax.axis_size(axis_name)
    here = lax.axis_index(axis_name)
    width = out_weight.shape[1] // count
    from_left = None
    from_right = None
    for step in range(1, count):
        right_shard = jnp.clip(here + count - step, 0, count - 1)
        left_shard = jnp.clip(here - count + step, 0, count - 1)
        if 2 * step <= count:
            shard = jnp.where(here < step, right_shard, left_shard)
            to_right = shard_product(gated, out_weight, shard, width)
            if step == 1:
                to_right, total_squares = lax.optimization_barrier((to_right, total_squares))
            else:
                to_right = lax.optimization_barrier(to_right)
            to_left = to_right
        else:
            to_right = shard_product(gated, out_weight, right_shard, width)
            to_left = shard_product(gated, out_weight, left_shard, width)
            if step == 1:
                to_right, to_left, total_squares = lax.optimization_barrier(
                    (to_right, to_left, total_squares)
                )
            else:
                to_right, to_left = lax.optimization_barrier((to_right, to_left))
        if from_left is not None:
            to_right = to_right + from_left
            to_left = to_left + from_right
        right_pairs = [(i, i + 1) for i in range(step) if i + 1 < count]
        left_pairs = [(i, i - 1) for i in range(count - step, count) if i >= 1]
        from_left = lax.ppermute(to_right.astype(jnp.bfloat16), axis_name, right_pairs)
        from_right = lax.ppermute(to_left.astype(jnp.bfloat16), axis_name, left_pairs)
        from_left = from_left.astype(jnp.float32)
        from_right = from_right.astype(jnp.float32)
    own = shard_product(gated, out_weight, here, width)
    scaling = lax.rsqrt(total_squares / (HEADS * HEAD_DIM) + 1e-06)
    if from_left is not None:
        own = own + from_left + from_right
    return own * scaling[:, None]


def body(queries, keys, values, gate_logits, out_weight):
    tokens_here = queries.shape[0]
    feature_count = queries.shape[1]
    heads_here = feature_count // HEAD_DIM
    block_rows = min(512, tokens_here)
    block_count = tokens_here // block_rows
    shape_blocks = (block_count, block_rows, heads_here, HEAD_DIM)
    active_q = activate(queries).reshape(shape_blocks)
    active_k = activate(keys).reshape(shape_blocks)
    active_v = activate(values).reshape(shape_blocks)
    block_states = jnp.einsum(
        "nshd,nshe->nhde", active_k, active_v, preferred_element_type=jnp.float32
    )
    span_total = jnp.sum(block_states, axis=0)
    earlier_local = jnp.cumsum(block_states, axis=0) - block_states
    prefix = exclusive_prefix(span_total, "seq")
    causal_mask = jnp.tril(jnp.ones((block_rows, block_rows), jnp.float32))
    scores = jnp.einsum("nthd,nshd->nhts", active_q, active_k, preferred_element_type=jnp.float32)
    scores = (scores * causal_mask).astype(jnp.bfloat16)
    within_block = jnp.einsum(
        "nhts,nshd->nthd", scores, active_v, preferred_element_type=jnp.float32
    )
    within_block, prefix = lax.optimization_barrier((within_block, prefix))
    before = (prefix[None] + earlier_local).astype(jnp.bfloat16)
    from_state = jnp.einsum("nthd,nhde->nthe", active_q, before, preferred_element_type=jnp.float32)
    attended = (within_block + from_state).reshape(tokens_here, feature_count)
    square_sums = jnp.sum(attended * attended, axis=-1)
    gate = jax.nn.sigmoid(gate_logits.astype(jnp.float32))
    gated = (attended * gate).astype(jnp.bfloat16)
    total_squares = butterfly_sum(square_sums, "head")
    reduced = line_reduce_scatter(gated, out_weight, "head", total_squares)
    return reduced.astype(jnp.bfloat16)


def solution(mesh):
    return jax.shard_map(
        body,
        mesh=mesh,
        in_specs=(
            P("seq", "head"),
            P("seq", "head"),
            P("seq", "head"),
            P("seq", "head"),
            P("head", None),
        ),
        out_specs=P("seq", "head"),
        check_vma=False,
    )
```

```python
import jax
import jax.numpy as jnp
from jax import lax
from jax.sharding import PartitionSpec as P

HEADS = 32
HEAD_DIM = 128


def activate(raw_input):
    return jax.nn.silu(raw_input.astype(jnp.float32)).astype(jnp.bfloat16)


def exclusive_prefix(span_total, axis_name, companion):
    count = lax.axis_size(axis_name)
    my_index = lax.axis_index(axis_name)
    if count & (count - 1):
        shards = lax.all_gather(
            span_total[None].astype(jnp.bfloat16), axis_name, axis=0, tiled=True
        ).astype(jnp.float32)
        positions = jnp.arange(count, dtype=jnp.int32)
        weights = (positions < my_index).astype(jnp.float32)
        return jnp.sum(shards * weights[:, None, None, None], axis=0), companion
    group_total = span_total
    prefix = jnp.zeros_like(span_total)
    bit = 1
    while bit < count:
        if bit * 2 == count and bit > 1:
            group_total, companion = lax.optimization_barrier((group_total, companion))
        pairs = [(i, i ^ bit) for i in range(count)]
        arrived = lax.ppermute(group_total.astype(jnp.bfloat16), axis_name, pairs)
        arrived = arrived.astype(jnp.float32)
        upper = ((my_index // bit) % 2).astype(jnp.float32)
        prefix = prefix + upper * arrived
        group_total = group_total + arrived
        bit *= 2
    return prefix, companion


def shard_product(gated, out_weight, shard, width):
    columns = lax.dynamic_slice_in_dim(out_weight, shard * width, width, axis=1)
    return jnp.dot(gated, columns, preferred_element_type=jnp.float32)


def butterfly_sum(values, axis_name):
    count = lax.axis_size(axis_name)
    if count & (count - 1):
        return lax.psum(values, axis_name)
    bit = 1
    while bit < count:
        values = values + lax.ppermute(values, axis_name, [(i, i ^ bit) for i in range(count)])
        bit *= 2
    return values


def line_reduce_scatter(gated, out_weight, axis_name, total_squares):
    count = lax.axis_size(axis_name)
    here = lax.axis_index(axis_name)
    width = out_weight.shape[1] // count
    from_left = None
    from_right = None
    for step in range(1, count):
        right_shard = jnp.clip(here + count - step, 0, count - 1)
        left_shard = jnp.clip(here - count + step, 0, count - 1)
        if 2 * step <= count:
            shard = jnp.where(here < step, right_shard, left_shard)
            to_right = shard_product(gated, out_weight, shard, width)
            if step == 1:
                to_right, total_squares = lax.optimization_barrier((to_right, total_squares))
            else:
                to_right = lax.optimization_barrier(to_right)
            to_left = to_right
        else:
            to_right = shard_product(gated, out_weight, right_shard, width)
            to_left = shard_product(gated, out_weight, left_shard, width)
            if step == 1:
                to_right, to_left, total_squares = lax.optimization_barrier(
                    (to_right, to_left, total_squares)
                )
            else:
                to_right, to_left = lax.optimization_barrier((to_right, to_left))
        if from_left is not None:
            to_right = to_right + from_left
            to_left = to_left + from_right
        right_pairs = [(i, i + 1) for i in range(step) if i + 1 < count]
        left_pairs = [(i, i - 1) for i in range(count - step, count) if i >= 1]
        from_left = lax.ppermute(to_right.astype(jnp.bfloat16), axis_name, right_pairs)
        from_right = lax.ppermute(to_left.astype(jnp.bfloat16), axis_name, left_pairs)
        from_left = from_left.astype(jnp.float32)
        from_right = from_right.astype(jnp.float32)
    own = shard_product(gated, out_weight, here, width)
    scaling = lax.rsqrt(total_squares / (HEADS * HEAD_DIM) + 1e-06)
    if from_left is not None:
        own = own + from_left + from_right
    return own * scaling[:, None]


def body(queries, keys, values, gate_logits, out_weight):
    tokens_here = queries.shape[0]
    feature_count = queries.shape[1]
    heads_here = feature_count // HEAD_DIM
    block_rows = min(512, tokens_here)
    block_count = tokens_here // block_rows
    shape_blocks = (block_count, block_rows, heads_here, HEAD_DIM)
    active_q = activate(queries).reshape(shape_blocks)
    active_k = activate(keys).reshape(shape_blocks)
    active_v = activate(values).reshape(shape_blocks)
    block_states = jnp.einsum(
        "nshd,nshe->nhde", active_k, active_v, preferred_element_type=jnp.float32
    )
    span_total = jnp.sum(block_states, axis=0)
    earlier_local = jnp.cumsum(block_states, axis=0) - block_states
    causal_mask = jnp.tril(jnp.ones((block_rows, block_rows), jnp.float32))
    scores = jnp.einsum("nthd,nshd->nhts", active_q, active_k, preferred_element_type=jnp.float32)
    scores = (scores * causal_mask).astype(jnp.bfloat16)
    within_block = jnp.einsum(
        "nhts,nshd->nthd", scores, active_v, preferred_element_type=jnp.float32
    )
    prefix, within_block = exclusive_prefix(span_total, "seq", within_block)
    within_block, prefix = lax.optimization_barrier((within_block, prefix))
    before = (prefix[None] + earlier_local).astype(jnp.bfloat16)
    from_state = jnp.einsum("nthd,nhde->nthe", active_q, before, preferred_element_type=jnp.float32)
    attended = (within_block + from_state).reshape(tokens_here, feature_count)
    square_sums = jnp.sum(attended * attended, axis=-1)
    gate = jax.nn.sigmoid(gate_logits.astype(jnp.float32))
    gated = (attended * gate).astype(jnp.bfloat16)
    total_squares = butterfly_sum(square_sums, "head")
    reduced = line_reduce_scatter(gated, out_weight, "head", total_squares)
    return reduced.astype(jnp.bfloat16)


def solution(mesh):
    return jax.shard_map(
        body,
        mesh=mesh,
        in_specs=(
            P("seq", "head"),
            P("seq", "head"),
            P("seq", "head"),
            P("seq", "head"),
            P("head", None),
        ),
        out_specs=P("seq", "head"),
        check_vma=False,
    )
```

```python
import jax
import jax.numpy as jnp
from jax import lax
from jax.sharding import PartitionSpec as P
from jax.experimental import pallas as pl

HEADS = 32
HEAD_DIM = 128


def activate(raw_input):
    return jax.nn.silu(raw_input.astype(jnp.float32)).astype(jnp.bfloat16)


def exclusive_prefix(span_total, axis_name, companion):
    count = lax.axis_size(axis_name)
    my_index = lax.axis_index(axis_name)
    if count & (count - 1):
        shards = lax.all_gather(
            span_total[None].astype(jnp.bfloat16), axis_name, axis=0, tiled=True
        ).astype(jnp.float32)
        positions = jnp.arange(count, dtype=jnp.int32)
        weights = (positions < my_index).astype(jnp.float32)
        return jnp.sum(shards * weights[:, None, None, None], axis=0), companion
    group_total = span_total
    prefix = jnp.zeros_like(span_total)
    bit = 1
    while bit < count:
        if bit * 2 == count and bit > 1:
            group_total, companion = lax.optimization_barrier((group_total, companion))
        pairs = [(i, i ^ bit) for i in range(count)]
        arrived = lax.ppermute(group_total.astype(jnp.bfloat16), axis_name, pairs)
        arrived = arrived.astype(jnp.float32)
        upper = ((my_index // bit) % 2).astype(jnp.float32)
        prefix = prefix + upper * arrived
        group_total = group_total + arrived
        bit *= 2
    return prefix, companion


def shard_product(gated, out_weight, shard, width):
    columns = lax.dynamic_slice_in_dim(out_weight, shard * width, width, axis=1)
    return jnp.dot(gated, columns, preferred_element_type=jnp.float32)


def butterfly_sum(values, axis_name):
    count = lax.axis_size(axis_name)
    if count & (count - 1):
        return lax.psum(values, axis_name)
    bit = 1
    while bit < count:
        values = values + lax.ppermute(values, axis_name, [(i, i ^ bit) for i in range(count)])
        bit *= 2
    return values


def line_reduce_scatter(gated, out_weight, axis_name, total_squares):
    count = lax.axis_size(axis_name)
    here = lax.axis_index(axis_name)
    width = out_weight.shape[1] // count
    from_left = None
    from_right = None
    for step in range(1, count):
        right_shard = jnp.clip(here + count - step, 0, count - 1)
        left_shard = jnp.clip(here - count + step, 0, count - 1)
        if 2 * step <= count:
            shard = jnp.where(here < step, right_shard, left_shard)
            to_right = shard_product(gated, out_weight, shard, width)
            if step == 1:
                to_right, total_squares = lax.optimization_barrier((to_right, total_squares))
            else:
                to_right = lax.optimization_barrier(to_right)
            to_left = to_right
        else:
            to_right = shard_product(gated, out_weight, right_shard, width)
            to_left = shard_product(gated, out_weight, left_shard, width)
            if step == 1:
                to_right, to_left, total_squares = lax.optimization_barrier(
                    (to_right, to_left, total_squares)
                )
            else:
                to_right, to_left = lax.optimization_barrier((to_right, to_left))
        if from_left is not None:
            to_right = to_right + from_left
            to_left = to_left + from_right
        right_pairs = [(i, i + 1) for i in range(step) if i + 1 < count]
        left_pairs = [(i, i - 1) for i in range(count - step, count) if i >= 1]
        from_left = lax.ppermute(to_right.astype(jnp.bfloat16), axis_name, right_pairs)
        from_right = lax.ppermute(to_left.astype(jnp.bfloat16), axis_name, left_pairs)
        from_left = from_left.astype(jnp.float32)
        from_right = from_right.astype(jnp.float32)
    own = shard_product(gated, out_weight, here, width)
    scaling = lax.rsqrt(total_squares / (HEADS * HEAD_DIM) + 1e-06)
    if from_left is not None:
        own = own + from_left + from_right
    return own * scaling[:, None]


def finish_kernel(query_ref, within_ref, gate_ref, state_ref, gated_ref, squares_ref):
    head = pl.program_id(0)
    attended = within_ref[...] + jnp.dot(
        query_ref[...], state_ref[0], preferred_element_type=jnp.float32
    )

    @pl.when(head == 0)
    def _():
        squares_ref[...] = jnp.zeros_like(squares_ref)

    squares_ref[...] += jnp.sum(attended * attended, axis=1, keepdims=True)
    gate = jax.nn.sigmoid(gate_ref[...].astype(jnp.float32))
    gated_ref[...] = (attended * gate).astype(jnp.bfloat16)


def finish(active_q, within, gate_logits, state):
    tokens, features = active_q.shape
    heads = features // HEAD_DIM
    column = pl.BlockSpec((tokens, HEAD_DIM), lambda h: (0, h))
    return pl.pallas_call(
        finish_kernel,
        grid=(heads,),
        in_specs=[
            column,
            column,
            column,
            pl.BlockSpec((1, HEAD_DIM, HEAD_DIM), lambda h: (h, 0, 0)),
        ],
        out_specs=[column, pl.BlockSpec((tokens, 1), lambda h: (0, 0))],
        out_shape=[
            jax.ShapeDtypeStruct((tokens, features), jnp.bfloat16),
            jax.ShapeDtypeStruct((tokens, 1), jnp.float32),
        ],
    )(active_q, within, gate_logits, state)


def body(queries, keys, values, gate_logits, out_weight):
    tokens_here = queries.shape[0]
    feature_count = queries.shape[1]
    heads_here = feature_count // HEAD_DIM
    block_rows = min(512, tokens_here)
    block_count = tokens_here // block_rows
    shape_blocks = (block_count, block_rows, heads_here, HEAD_DIM)
    active_q = activate(queries).reshape(shape_blocks)
    active_k = activate(keys).reshape(shape_blocks)
    active_v = activate(values).reshape(shape_blocks)
    block_states = jnp.einsum(
        "nshd,nshe->nhde", active_k, active_v, preferred_element_type=jnp.float32
    )
    span_total = jnp.sum(block_states, axis=0)
    earlier_local = jnp.cumsum(block_states, axis=0) - block_states
    causal_mask = jnp.tril(jnp.ones((block_rows, block_rows), jnp.float32))
    scores = jnp.einsum("nthd,nshd->nhts", active_q, active_k, preferred_element_type=jnp.float32)
    scores = (scores * causal_mask).astype(jnp.bfloat16)
    within_block = jnp.einsum(
        "nhts,nshd->nthd", scores, active_v, preferred_element_type=jnp.float32
    )
    within_rows = within_block.reshape(tokens_here, feature_count)
    prefix, within_rows = exclusive_prefix(span_total, "seq", within_rows)
    within_block, prefix = lax.optimization_barrier((within_block, prefix))
    before = (prefix[None] + earlier_local).astype(jnp.bfloat16)
    if block_count == 1:
        gated, square_sums = finish(
            active_q.reshape(tokens_here, feature_count),
            within_rows,
            gate_logits,
            before[0],
        )
        square_sums = square_sums[:, 0]
    else:
        from_state = jnp.einsum(
            "nthd,nhde->nthe", active_q, before, preferred_element_type=jnp.float32
        )
        attended = within_rows + from_state.reshape(tokens_here, feature_count)
        square_sums = jnp.sum(attended * attended, axis=-1)
        gate = jax.nn.sigmoid(gate_logits.astype(jnp.float32))
        gated = (attended * gate).astype(jnp.bfloat16)
    total_squares = butterfly_sum(square_sums, "head")
    reduced = line_reduce_scatter(gated, out_weight, "head", total_squares)
    return reduced.astype(jnp.bfloat16)


def solution(mesh):
    return jax.shard_map(
        body,
        mesh=mesh,
        in_specs=(
            P("seq", "head"),
            P("seq", "head"),
            P("seq", "head"),
            P("seq", "head"),
            P("head", None),
        ),
        out_specs=P("seq", "head"),
        check_vma=False,
    )
```

```python
import jax
import jax.numpy as jnp
from jax import lax
from jax.sharding import PartitionSpec as P
from jax.experimental import pallas as pl

HEADS = 32
HEAD_DIM = 128


def activate(raw_input):
    return jax.nn.silu(raw_input.astype(jnp.float32)).astype(jnp.bfloat16)


def exclusive_prefix(span_total, axis_name, companion):
    count = lax.axis_size(axis_name)
    my_index = lax.axis_index(axis_name)
    if count & (count - 1):
        shards = lax.all_gather(
            span_total[None].astype(jnp.bfloat16), axis_name, axis=0, tiled=True
        ).astype(jnp.float32)
        positions = jnp.arange(count, dtype=jnp.int32)
        weights = (positions < my_index).astype(jnp.float32)
        return jnp.sum(shards * weights[:, None, None, None], axis=0), companion
    group_total = span_total
    prefix = jnp.zeros_like(span_total)
    bit = 1
    while bit < count:
        if bit * 2 == count and bit > 1:
            group_total, companion = lax.optimization_barrier((group_total, companion))
        pairs = [(i, i ^ bit) for i in range(count)]
        arrived = lax.ppermute(group_total.astype(jnp.bfloat16), axis_name, pairs)
        arrived = arrived.astype(jnp.float32)
        upper = ((my_index // bit) % 2).astype(jnp.float32)
        prefix = prefix + upper * arrived
        group_total = group_total + arrived
        bit *= 2
    return prefix, companion


def shard_product(gated, out_weight, shard, width):
    columns = lax.dynamic_slice_in_dim(out_weight, shard * width, width, axis=1)
    return jnp.dot(gated, columns, preferred_element_type=jnp.float32)


def butterfly_sum(values, axis_name):
    count = lax.axis_size(axis_name)
    if count & (count - 1):
        return lax.psum(values, axis_name)
    bit = 1
    while bit < count:
        values = values + lax.ppermute(values, axis_name, [(i, i ^ bit) for i in range(count)])
        bit *= 2
    return values


def line_reduce_scatter(gated, out_weight, axis_name, total_squares):
    count = lax.axis_size(axis_name)
    here = lax.axis_index(axis_name)
    width = out_weight.shape[1] // count
    from_left = None
    from_right = None
    for step in range(1, count):
        right_shard = jnp.clip(here + count - step, 0, count - 1)
        left_shard = jnp.clip(here - count + step, 0, count - 1)
        if 2 * step <= count:
            shard = jnp.where(here < step, right_shard, left_shard)
            to_right = shard_product(gated, out_weight, shard, width)
            if step == 1:
                to_right, total_squares = lax.optimization_barrier((to_right, total_squares))
            else:
                to_right = lax.optimization_barrier(to_right)
            to_left = to_right
        else:
            to_right = shard_product(gated, out_weight, right_shard, width)
            to_left = shard_product(gated, out_weight, left_shard, width)
            if step == 1:
                to_right, to_left, total_squares = lax.optimization_barrier(
                    (to_right, to_left, total_squares)
                )
            else:
                to_right, to_left = lax.optimization_barrier((to_right, to_left))
        if from_left is not None:
            to_right = to_right + from_left
            to_left = to_left + from_right
        right_pairs = [(i, i + 1) for i in range(step) if i + 1 < count]
        left_pairs = [(i, i - 1) for i in range(count - step, count) if i >= 1]
        from_left = lax.ppermute(to_right.astype(jnp.bfloat16), axis_name, right_pairs)
        from_right = lax.ppermute(to_left.astype(jnp.bfloat16), axis_name, left_pairs)
        from_left = from_left.astype(jnp.float32)
        from_right = from_right.astype(jnp.float32)
    own = shard_product(gated, out_weight, here, width)
    scaling = lax.rsqrt(total_squares / (HEADS * HEAD_DIM) + 1e-06)
    if from_left is not None:
        own = own + from_left + from_right
    return own * scaling


def finish_kernel(query_ref, within_ref, gate_ref, state_ref, gated_ref, squares_ref):
    step = pl.program_id(0)

    @pl.when(step == 0)
    def _():
        squares_ref[...] = jnp.zeros_like(squares_ref)

    total = jnp.zeros(squares_ref.shape, jnp.float32)
    for head in range(state_ref.shape[0]):
        cols = slice(head * HEAD_DIM, (head + 1) * HEAD_DIM)
        attended = within_ref[:, cols] + jnp.dot(
            query_ref[:, cols], state_ref[head], preferred_element_type=jnp.float32
        )
        total = total + jnp.sum(attended * attended, axis=1, keepdims=True)
        gate = jax.nn.sigmoid(gate_ref[:, cols].astype(jnp.float32))
        gated_ref[:, cols] = (attended * gate).astype(jnp.bfloat16)
    squares_ref[...] += total


def finish(active_q, within, gate_logits, state):
    tokens, features = active_q.shape
    heads = features // HEAD_DIM
    group = 4 if heads % 4 == 0 else 1
    column = pl.BlockSpec((tokens, group * HEAD_DIM), lambda g: (0, g))
    return pl.pallas_call(
        finish_kernel,
        grid=(heads // group,),
        in_specs=[
            column,
            column,
            column,
            pl.BlockSpec((group, HEAD_DIM, HEAD_DIM), lambda g: (g, 0, 0)),
        ],
        out_specs=[column, pl.BlockSpec((tokens, 1), lambda g: (0, 0))],
        out_shape=[
            jax.ShapeDtypeStruct((tokens, features), jnp.bfloat16),
            jax.ShapeDtypeStruct((tokens, 1), jnp.float32),
        ],
    )(active_q, within, gate_logits, state)


def body(queries, keys, values, gate_logits, out_weight):
    tokens_here = queries.shape[0]
    feature_count = queries.shape[1]
    heads_here = feature_count // HEAD_DIM
    block_rows = min(512, tokens_here)
    block_count = tokens_here // block_rows
    shape_blocks = (block_count, block_rows, heads_here, HEAD_DIM)
    active_q = activate(queries).reshape(shape_blocks)
    active_k = activate(keys).reshape(shape_blocks)
    active_v = activate(values).reshape(shape_blocks)
    block_states = jnp.einsum(
        "nshd,nshe->nhde", active_k, active_v, preferred_element_type=jnp.float32
    )
    span_total = jnp.sum(block_states, axis=0)
    earlier_local = jnp.cumsum(block_states, axis=0) - block_states
    causal_mask = jnp.tril(jnp.ones((block_rows, block_rows), jnp.float32))
    scores = jnp.einsum("nthd,nshd->nhts", active_q, active_k, preferred_element_type=jnp.float32)
    scores = (scores * causal_mask).astype(jnp.bfloat16)
    within_block = jnp.einsum(
        "nhts,nshd->nthd", scores, active_v, preferred_element_type=jnp.float32
    )
    within_rows = within_block.reshape(tokens_here, feature_count)
    prefix, within_rows = exclusive_prefix(span_total, "seq", within_rows)
    within_block, prefix = lax.optimization_barrier((within_block, prefix))
    before = (prefix[None] + earlier_local).astype(jnp.bfloat16)
    if block_count == 1:
        gated, square_sums = finish(
            active_q.reshape(tokens_here, feature_count),
            within_rows,
            gate_logits,
            before[0],
        )
    else:
        from_state = jnp.einsum(
            "nthd,nhde->nthe", active_q, before, preferred_element_type=jnp.float32
        )
        attended = within_rows + from_state.reshape(tokens_here, feature_count)
        square_sums = jnp.sum(attended * attended, axis=-1, keepdims=True)
        gate = jax.nn.sigmoid(gate_logits.astype(jnp.float32))
        gated = (attended * gate).astype(jnp.bfloat16)
    total_squares = butterfly_sum(square_sums, "head")
    reduced = line_reduce_scatter(gated, out_weight, "head", total_squares)
    return reduced.astype(jnp.bfloat16)


def solution(mesh):
    return jax.shard_map(
        body,
        mesh=mesh,
        in_specs=(
            P("seq", "head"),
            P("seq", "head"),
            P("seq", "head"),
            P("seq", "head"),
            P("head", None),
        ),
        out_specs=P("seq", "head"),
        check_vma=False,
    )
```

```python
import jax
import jax.numpy as jnp
from jax import lax
from jax.sharding import PartitionSpec as P
from jax.experimental import pallas as pl

HEADS = 32
HEAD_DIM = 128


def activate(raw_input):
    return jax.nn.silu(raw_input.astype(jnp.float32)).astype(jnp.bfloat16)


def exclusive_prefix(span_total, axis_name, companion):
    count = lax.axis_size(axis_name)
    my_index = lax.axis_index(axis_name)
    if count & (count - 1):
        shards = lax.all_gather(
            span_total[None].astype(jnp.bfloat16), axis_name, axis=0, tiled=True
        ).astype(jnp.float32)
        positions = jnp.arange(count, dtype=jnp.int32)
        weights = (positions < my_index).astype(jnp.float32)
        return jnp.sum(shards * weights[:, None, None, None], axis=0), companion
    group_total = span_total
    prefix = jnp.zeros_like(span_total)
    bit = 1
    while bit < count:
        if bit * 2 == count and bit > 1:
            group_total, companion = lax.optimization_barrier((group_total, companion))
        pairs = [(i, i ^ bit) for i in range(count)]
        arrived = lax.ppermute(group_total.astype(jnp.bfloat16), axis_name, pairs)
        arrived = arrived.astype(jnp.float32)
        upper = ((my_index // bit) % 2).astype(jnp.float32)
        prefix = prefix + upper * arrived
        group_total = group_total + arrived
        bit *= 2
    return prefix, companion


def shard_product(gated, out_weight, shard, width):
    columns = lax.dynamic_slice_in_dim(out_weight, shard * width, width, axis=1)
    return jnp.dot(gated, columns, preferred_element_type=jnp.float32)


def butterfly_sum(values, axis_name):
    count = lax.axis_size(axis_name)
    if count & (count - 1):
        return lax.psum(values, axis_name)
    bit = 1
    while bit < count:
        values = values + lax.ppermute(values, axis_name, [(i, i ^ bit) for i in range(count)])
        bit *= 2
    return values


def line_reduce_scatter(gated, out_weight, axis_name, total_squares):
    count = lax.axis_size(axis_name)
    here = lax.axis_index(axis_name)
    width = out_weight.shape[1] // count
    from_left = None
    from_right = None
    for step in range(1, count):
        right_shard = jnp.clip(here + count - step, 0, count - 1)
        left_shard = jnp.clip(here - count + step, 0, count - 1)
        if 2 * step <= count:
            shard = jnp.where(here < step, right_shard, left_shard)
            to_right = shard_product(gated, out_weight, shard, width)
            if step == 1:
                to_right, total_squares = lax.optimization_barrier((to_right, total_squares))
            else:
                to_right = lax.optimization_barrier(to_right)
            to_left = to_right
        else:
            to_right = shard_product(gated, out_weight, right_shard, width)
            to_left = shard_product(gated, out_weight, left_shard, width)
            if step == 1:
                to_right, to_left, total_squares = lax.optimization_barrier(
                    (to_right, to_left, total_squares)
                )
            else:
                to_right, to_left = lax.optimization_barrier((to_right, to_left))
        if from_left is not None:
            to_right = to_right + from_left
            to_left = to_left + from_right
        right_pairs = [(i, i + 1) for i in range(step) if i + 1 < count]
        left_pairs = [(i, i - 1) for i in range(count - step, count) if i >= 1]
        from_left = lax.ppermute(to_right.astype(jnp.bfloat16), axis_name, right_pairs)
        from_right = lax.ppermute(to_left.astype(jnp.bfloat16), axis_name, left_pairs)
        from_left = from_left.astype(jnp.float32)
        from_right = from_right.astype(jnp.float32)
    own = shard_product(gated, out_weight, here, width)
    scaling = lax.rsqrt(total_squares / (HEADS * HEAD_DIM) + 1e-06)
    if from_left is not None:
        own = own + from_left + from_right
    return own * scaling[:, None]


def finish_kernel(query_ref, within_ref, gate_ref, state_ref, gated_ref, squares_ref):
    step = pl.program_id(0)

    @pl.when(step == 0)
    def _():
        squares_ref[...] = jnp.zeros_like(squares_ref)

    total = jnp.zeros(squares_ref.shape, jnp.float32)
    for head in range(state_ref.shape[0]):
        cols = slice(head * HEAD_DIM, (head + 1) * HEAD_DIM)
        attended = within_ref[:, cols] + jnp.dot(
            query_ref[:, cols], state_ref[head], preferred_element_type=jnp.float32
        )
        total = total + jnp.sum(attended * attended, axis=1, keepdims=True)
        gate = jax.nn.sigmoid(gate_ref[:, cols].astype(jnp.float32))
        gated_ref[:, cols] = (attended * gate).astype(jnp.bfloat16)
    squares_ref[...] += total


def finish(active_q, within, gate_logits, state):
    tokens, features = active_q.shape
    heads = features // HEAD_DIM
    group = 4 if heads % 4 == 0 else 1
    column = pl.BlockSpec((tokens, group * HEAD_DIM), lambda g: (0, g))
    return pl.pallas_call(
        finish_kernel,
        grid=(heads // group,),
        in_specs=[
            column,
            column,
            column,
            pl.BlockSpec((group, HEAD_DIM, HEAD_DIM), lambda g: (g, 0, 0)),
        ],
        out_specs=[column, pl.BlockSpec((tokens, 1), lambda g: (0, 0))],
        out_shape=[
            jax.ShapeDtypeStruct((tokens, features), jnp.bfloat16),
            jax.ShapeDtypeStruct((tokens, 1), jnp.float32),
        ],
    )(active_q, within, gate_logits, state)


def body(queries, keys, values, gate_logits, out_weight):
    tokens_here = queries.shape[0]
    feature_count = queries.shape[1]
    heads_here = feature_count // HEAD_DIM
    block_rows = min(512, tokens_here)
    block_count = tokens_here // block_rows
    shape_blocks = (block_count, block_rows, heads_here, HEAD_DIM)
    active_q = activate(queries).reshape(shape_blocks)
    active_k = activate(keys).reshape(shape_blocks)
    active_v = activate(values).reshape(shape_blocks)
    block_states = jnp.einsum(
        "nshd,nshe->nhde", active_k, active_v, preferred_element_type=jnp.float32
    )
    span_total = jnp.sum(block_states, axis=0)
    earlier_local = jnp.cumsum(block_states, axis=0) - block_states
    causal_mask = jnp.tril(jnp.ones((block_rows, block_rows), jnp.float32))
    scores = jnp.einsum("nthd,nshd->nhts", active_q, active_k, preferred_element_type=jnp.float32)
    scores = (scores * causal_mask).astype(jnp.bfloat16)
    within_block = jnp.einsum(
        "nhts,nshd->nthd", scores, active_v, preferred_element_type=jnp.float32
    )
    within_rows = within_block.reshape(tokens_here, feature_count)
    prefix, within_rows = exclusive_prefix(span_total, "seq", within_rows)
    within_block, prefix = lax.optimization_barrier((within_block, prefix))
    before = (prefix[None] + earlier_local).astype(jnp.bfloat16)
    if block_count == 1:
        gated, square_sums = finish(
            active_q.reshape(tokens_here, feature_count),
            within_rows,
            gate_logits,
            before[0],
        )
        square_sums = square_sums[:, 0]
    else:
        from_state = jnp.einsum(
            "nthd,nhde->nthe", active_q, before, preferred_element_type=jnp.float32
        )
        attended = within_rows + from_state.reshape(tokens_here, feature_count)
        square_sums = jnp.sum(attended * attended, axis=-1)
        gate = jax.nn.sigmoid(gate_logits.astype(jnp.float32))
        gated = (attended * gate).astype(jnp.bfloat16)
    total_squares = butterfly_sum(square_sums, "head")
    reduced = line_reduce_scatter(gated, out_weight, "head", total_squares)
    return reduced.astype(jnp.bfloat16)


def solution(mesh):
    return jax.shard_map(
        body,
        mesh=mesh,
        in_specs=(
            P("seq", "head"),
            P("seq", "head"),
            P("seq", "head"),
            P("seq", "head"),
            P("head", None),
        ),
        out_specs=P("seq", "head"),
        check_vma=False,
    )
```

```python
import jax
import jax.numpy as jnp
from jax import lax
from jax.sharding import PartitionSpec as P

HEADS = 32
HEAD_DIM = 128


def activate(raw_input):
    return jax.nn.silu(raw_input.astype(jnp.float32)).astype(jnp.bfloat16)


def exclusive_prefix(span_total, axis_name, companion):
    count = lax.axis_size(axis_name)
    my_index = lax.axis_index(axis_name)
    if count & (count - 1):
        shards = lax.all_gather(
            span_total[None].astype(jnp.bfloat16), axis_name, axis=0, tiled=True
        ).astype(jnp.float32)
        positions = jnp.arange(count, dtype=jnp.int32)
        weights = (positions < my_index).astype(jnp.float32)
        return jnp.sum(shards * weights[:, None, None, None], axis=0), companion
    group_total = span_total
    prefix = jnp.zeros_like(span_total)
    bit = 1
    while bit < count:
        if bit * 2 == count and bit > 1:
            group_total, companion = lax.optimization_barrier((group_total, companion))
        pairs = [(i, i ^ bit) for i in range(count)]
        arrived = lax.ppermute(group_total.astype(jnp.bfloat16), axis_name, pairs)
        arrived = arrived.astype(jnp.float32)
        upper = ((my_index // bit) % 2).astype(jnp.float32)
        prefix = prefix + upper * arrived
        group_total = group_total + arrived
        bit *= 2
    return prefix, companion


def shard_product(gated, out_weight, shard, width):
    columns = lax.dynamic_slice_in_dim(out_weight, shard * width, width, axis=1)
    return jnp.dot(gated, columns, preferred_element_type=jnp.float32)


def butterfly_sum(values, axis_name):
    count = lax.axis_size(axis_name)
    if count & (count - 1):
        return lax.psum(values, axis_name)
    bit = 1
    while bit < count:
        values = values + lax.ppermute(values, axis_name, [(i, i ^ bit) for i in range(count)])
        bit *= 2
    return values


def line_reduce_scatter(gated, out_weight, axis_name, total_squares):
    count = lax.axis_size(axis_name)
    here = lax.axis_index(axis_name)
    width = out_weight.shape[1] // count
    from_left = None
    from_right = None
    for step in range(1, count):
        right_shard = jnp.clip(here + count - step, 0, count - 1)
        left_shard = jnp.clip(here - count + step, 0, count - 1)
        if 2 * step <= count:
            shard = jnp.where(here < step, right_shard, left_shard)
            product = shard_product(gated, out_weight, shard, width).astype(jnp.bfloat16)
            if step == 1:
                product, total_squares = lax.optimization_barrier((product, total_squares))
            else:
                product = lax.optimization_barrier(product)
            to_right = product.astype(jnp.float32)
            if from_left is not None:
                to_right = to_right + from_left + from_right
            to_right = to_right.astype(jnp.bfloat16)
            to_left = to_right
        else:
            to_right = shard_product(gated, out_weight, right_shard, width).astype(jnp.bfloat16)
            to_left = shard_product(gated, out_weight, left_shard, width).astype(jnp.bfloat16)
            if step == 1:
                to_right, to_left, total_squares = lax.optimization_barrier(
                    (to_right, to_left, total_squares)
                )
            else:
                to_right, to_left = lax.optimization_barrier((to_right, to_left))
            if from_left is not None:
                to_right = (to_right.astype(jnp.float32) + from_left).astype(jnp.bfloat16)
                to_left = (to_left.astype(jnp.float32) + from_right).astype(jnp.bfloat16)
        right_pairs = [(i, i + 1) for i in range(step) if i + 1 < count]
        left_pairs = [(i, i - 1) for i in range(count - step, count) if i >= 1]
        from_left = lax.ppermute(to_right, axis_name, right_pairs).astype(jnp.float32)
        from_right = lax.ppermute(to_left, axis_name, left_pairs).astype(jnp.float32)
    own = shard_product(gated, out_weight, here, width).astype(jnp.bfloat16)
    own = own.astype(jnp.float32)
    scaling = lax.rsqrt(total_squares / (HEADS * HEAD_DIM) + 1e-06)
    if from_left is not None:
        own = own + from_left + from_right
    return own * scaling[:, None]


def body(queries, keys, values, gate_logits, out_weight):
    tokens_here = queries.shape[0]
    feature_count = queries.shape[1]
    heads_here = feature_count // HEAD_DIM
    block_rows = min(512, tokens_here)
    block_count = tokens_here // block_rows
    shape_blocks = (block_count, block_rows, heads_here, HEAD_DIM)
    active_q = activate(queries).reshape(shape_blocks)
    active_k = activate(keys).reshape(shape_blocks)
    active_v = activate(values).reshape(shape_blocks)
    block_states = jnp.einsum(
        "nshd,nshe->nhde", active_k, active_v, preferred_element_type=jnp.float32
    )
    span_total = jnp.sum(block_states, axis=0)
    earlier_local = jnp.cumsum(block_states, axis=0) - block_states
    causal_mask = jnp.tril(jnp.ones((block_rows, block_rows), jnp.float32))
    scores = jnp.einsum("nthd,nshd->nhts", active_q, active_k, preferred_element_type=jnp.float32)
    scores = (scores * causal_mask).astype(jnp.bfloat16)
    within_block = jnp.einsum(
        "nhts,nshd->nthd", scores, active_v, preferred_element_type=jnp.float32
    )
    prefix, within_block = exclusive_prefix(span_total, "seq", within_block)
    within_block, prefix = lax.optimization_barrier((within_block, prefix))
    before = (prefix[None] + earlier_local).astype(jnp.bfloat16)
    from_state = jnp.einsum("nthd,nhde->nthe", active_q, before, preferred_element_type=jnp.float32)
    attended = (within_block + from_state).reshape(tokens_here, feature_count)
    square_sums = jnp.sum(attended * attended, axis=-1)
    gate = jax.nn.sigmoid(gate_logits.astype(jnp.float32))
    gated = (attended * gate).astype(jnp.bfloat16)
    total_squares = butterfly_sum(square_sums, "head")
    reduced = line_reduce_scatter(gated, out_weight, "head", total_squares)
    return reduced.astype(jnp.bfloat16)


def solution(mesh):
    return jax.shard_map(
        body,
        mesh=mesh,
        in_specs=(
            P("seq", "head"),
            P("seq", "head"),
            P("seq", "head"),
            P("seq", "head"),
            P("head", None),
        ),
        out_specs=P("seq", "head"),
        check_vma=False,
    )
```

```python
import jax
import jax.numpy as jnp
from jax import lax
from jax.sharding import PartitionSpec as P

HEADS = 32
HEAD_DIM = 128


def activate(raw_input):
    return jax.nn.silu(raw_input.astype(jnp.float32)).astype(jnp.bfloat16)


def exclusive_prefix(span_total, axis_name, companion):
    count = lax.axis_size(axis_name)
    my_index = lax.axis_index(axis_name)
    if count & (count - 1):
        shards = lax.all_gather(
            span_total[None].astype(jnp.bfloat16), axis_name, axis=0, tiled=True
        ).astype(jnp.float32)
        positions = jnp.arange(count, dtype=jnp.int32)
        weights = (positions < my_index).astype(jnp.float32)
        return jnp.sum(shards * weights[:, None, None, None], axis=0), companion
    group_total = span_total
    prefix = jnp.zeros_like(span_total)
    bit = 1
    if count % 4 == 0 and count > 4:
        sent = span_total.astype(jnp.bfloat16)
        low = my_index % 4
        for partner in range(1, 4):
            pairs = [(i, i ^ partner) for i in range(count)]
            arrived = lax.ppermute(sent, axis_name, pairs).astype(jnp.float32)
            earlier = ((low ^ partner) < low).astype(jnp.float32)
            prefix = prefix + earlier * arrived
            group_total = group_total + arrived
        bit = 4
    while bit < count:
        if bit * 2 == count and bit > 1:
            group_total, companion = lax.optimization_barrier((group_total, companion))
        pairs = [(i, i ^ bit) for i in range(count)]
        arrived = lax.ppermute(group_total.astype(jnp.bfloat16), axis_name, pairs)
        arrived = arrived.astype(jnp.float32)
        upper = ((my_index // bit) % 2).astype(jnp.float32)
        prefix = prefix + upper * arrived
        group_total = group_total + arrived
        bit *= 2
    return prefix, companion


def shard_product(gated, out_weight, shard, width):
    columns = lax.dynamic_slice_in_dim(out_weight, shard * width, width, axis=1)
    return jnp.dot(gated, columns, preferred_element_type=jnp.float32)


def butterfly_sum(values, axis_name):
    count = lax.axis_size(axis_name)
    if count & (count - 1):
        return lax.psum(values, axis_name)
    bit = 1
    while bit < count:
        values = values + lax.ppermute(values, axis_name, [(i, i ^ bit) for i in range(count)])
        bit *= 2
    return values


def line_reduce_scatter(gated, out_weight, axis_name, total_squares):
    count = lax.axis_size(axis_name)
    here = lax.axis_index(axis_name)
    width = out_weight.shape[1] // count
    from_left = None
    from_right = None
    for step in range(1, count):
        right_shard = jnp.clip(here + count - step, 0, count - 1)
        left_shard = jnp.clip(here - count + step, 0, count - 1)
        if 2 * step <= count:
            shard = jnp.where(here < step, right_shard, left_shard)
            product = shard_product(gated, out_weight, shard, width).astype(jnp.bfloat16)
            if step == 1:
                product, total_squares = lax.optimization_barrier((product, total_squares))
            else:
                product = lax.optimization_barrier(product)
            to_right = product.astype(jnp.float32)
            if from_left is not None:
                to_right = to_right + from_left + from_right
            to_right = to_right.astype(jnp.bfloat16)
            to_left = to_right
        else:
            to_right = shard_product(gated, out_weight, right_shard, width).astype(jnp.bfloat16)
            to_left = shard_product(gated, out_weight, left_shard, width).astype(jnp.bfloat16)
            if step == 1:
                to_right, to_left, total_squares = lax.optimization_barrier(
                    (to_right, to_left, total_squares)
                )
            else:
                to_right, to_left = lax.optimization_barrier((to_right, to_left))
            if from_left is not None:
                to_right = (to_right.astype(jnp.float32) + from_left).astype(jnp.bfloat16)
                to_left = (to_left.astype(jnp.float32) + from_right).astype(jnp.bfloat16)
        right_pairs = [(i, i + 1) for i in range(step) if i + 1 < count]
        left_pairs = [(i, i - 1) for i in range(count - step, count) if i >= 1]
        from_left = lax.ppermute(to_right, axis_name, right_pairs).astype(jnp.float32)
        from_right = lax.ppermute(to_left, axis_name, left_pairs).astype(jnp.float32)
    own = shard_product(gated, out_weight, here, width).astype(jnp.bfloat16)
    own = own.astype(jnp.float32)
    scaling = lax.rsqrt(total_squares / (HEADS * HEAD_DIM) + 1e-06)
    if from_left is not None:
        own = own + from_left + from_right
    return own * scaling[:, None]


def body(queries, keys, values, gate_logits, out_weight):
    tokens_here = queries.shape[0]
    feature_count = queries.shape[1]
    heads_here = feature_count // HEAD_DIM
    block_rows = min(512, tokens_here)
    block_count = tokens_here // block_rows
    shape_blocks = (block_count, block_rows, heads_here, HEAD_DIM)
    active_q = activate(queries).reshape(shape_blocks)
    active_k = activate(keys).reshape(shape_blocks)
    active_v = activate(values).reshape(shape_blocks)
    block_states = jnp.einsum(
        "nshd,nshe->nhde", active_k, active_v, preferred_element_type=jnp.float32
    )
    span_total = jnp.sum(block_states, axis=0)
    earlier_local = jnp.cumsum(block_states, axis=0) - block_states
    causal_mask = jnp.tril(jnp.ones((block_rows, block_rows), jnp.float32))
    scores = jnp.einsum("nthd,nshd->nhts", active_q, active_k, preferred_element_type=jnp.float32)
    scores = (scores * causal_mask).astype(jnp.bfloat16)
    within_block = jnp.einsum(
        "nhts,nshd->nthd", scores, active_v, preferred_element_type=jnp.float32
    )
    prefix, within_block = exclusive_prefix(span_total, "seq", within_block)
    within_block, prefix = lax.optimization_barrier((within_block, prefix))
    before = (prefix[None] + earlier_local).astype(jnp.bfloat16)
    from_state = jnp.einsum("nthd,nhde->nthe", active_q, before, preferred_element_type=jnp.float32)
    attended = (within_block + from_state).reshape(tokens_here, feature_count)
    square_sums = jnp.sum(attended * attended, axis=-1)
    gate = jax.nn.sigmoid(gate_logits.astype(jnp.float32))
    gated = (attended * gate).astype(jnp.bfloat16)
    total_squares = butterfly_sum(square_sums, "head")
    reduced = line_reduce_scatter(gated, out_weight, "head", total_squares)
    return reduced.astype(jnp.bfloat16)


def solution(mesh):
    return jax.shard_map(
        body,
        mesh=mesh,
        in_specs=(
            P("seq", "head"),
            P("seq", "head"),
            P("seq", "head"),
            P("seq", "head"),
            P("head", None),
        ),
        out_specs=P("seq", "head"),
        check_vma=False,
    )
```

```python
import jax
import jax.numpy as jnp
from jax import lax
from jax.sharding import PartitionSpec as P

HEADS = 32
HEAD_DIM = 128


def activate(raw_input):
    return jax.nn.silu(raw_input.astype(jnp.float32)).astype(jnp.bfloat16)


def exclusive_prefix(span_total, axis_name, companion):
    count = lax.axis_size(axis_name)
    my_index = lax.axis_index(axis_name)
    if count & (count - 1):
        shards = lax.all_gather(
            span_total[None].astype(jnp.bfloat16), axis_name, axis=0, tiled=True
        ).astype(jnp.float32)
        positions = jnp.arange(count, dtype=jnp.int32)
        weights = (positions < my_index).astype(jnp.float32)
        return jnp.sum(shards * weights[:, None, None, None], axis=0), companion
    group_total = span_total
    prefix = jnp.zeros_like(span_total)
    bit = 1
    while bit < count:
        if bit * 2 == count and bit > 1:
            group_total, companion = lax.optimization_barrier((group_total, companion))
        pairs = [(i, i ^ bit) for i in range(count)]
        arrived = lax.ppermute(group_total.astype(jnp.bfloat16), axis_name, pairs)
        arrived = arrived.astype(jnp.float32)
        upper = ((my_index // bit) % 2).astype(jnp.float32)
        prefix = prefix + upper * arrived
        group_total = group_total + arrived
        bit *= 2
    return prefix, companion


def shard_product(gated, out_weight, shard, width):
    columns = lax.dynamic_slice_in_dim(out_weight, shard * width, width, axis=1)
    return jnp.dot(gated, columns, preferred_element_type=jnp.float32)


def butterfly_sum(values, axis_name):
    count = lax.axis_size(axis_name)
    if count & (count - 1):
        return lax.psum(values, axis_name)
    bit = 1
    while bit < count:
        values = values + lax.ppermute(values, axis_name, [(i, i ^ bit) for i in range(count)])
        bit *= 2
    return values


def line_reduce_scatter(gated, out_weight, axis_name, total_squares):
    count = lax.axis_size(axis_name)
    here = lax.axis_index(axis_name)
    width = out_weight.shape[1] // count
    from_left = None
    from_right = None
    for step in range(1, count):
        right_shard = jnp.clip(here + count - step, 0, count - 1)
        left_shard = jnp.clip(here - count + step, 0, count - 1)
        if 2 * step <= count:
            shard = jnp.where(here < step, right_shard, left_shard)
            product = shard_product(gated, out_weight, shard, width).astype(jnp.bfloat16)
            if step == 1:
                product, total_squares = lax.optimization_barrier((product, total_squares))
            else:
                product = lax.optimization_barrier(product)
            to_right = product.astype(jnp.float32)
            if from_left is not None:
                to_right = to_right + from_left + from_right
            to_right = to_right.astype(jnp.bfloat16)
            to_left = to_right
        else:
            to_right = shard_product(gated, out_weight, right_shard, width).astype(jnp.bfloat16)
            to_left = shard_product(gated, out_weight, left_shard, width).astype(jnp.bfloat16)
            if step == 1:
                to_right, to_left, total_squares = lax.optimization_barrier(
                    (to_right, to_left, total_squares)
                )
            else:
                to_right, to_left = lax.optimization_barrier((to_right, to_left))
            if from_left is not None:
                to_right = (to_right.astype(jnp.float32) + from_left).astype(jnp.bfloat16)
                to_left = (to_left.astype(jnp.float32) + from_right).astype(jnp.bfloat16)
        right_pairs = [(i, i + 1) for i in range(step) if i + 1 < count]
        left_pairs = [(i, i - 1) for i in range(count - step, count) if i >= 1]
        from_left = lax.ppermute(to_right, axis_name, right_pairs).astype(jnp.float32)
        from_right = lax.ppermute(to_left, axis_name, left_pairs).astype(jnp.float32)
    own = shard_product(gated, out_weight, here, width).astype(jnp.bfloat16)
    own = own.astype(jnp.float32)
    scaling = lax.rsqrt(total_squares / (HEADS * HEAD_DIM) + 1e-06)
    if from_left is not None:
        own = own + from_left + from_right
    return own * scaling[:, None]


def body(queries, keys, values, gate_logits, out_weight):
    tokens_here = queries.shape[0]
    feature_count = queries.shape[1]
    heads_here = feature_count // HEAD_DIM
    block_rows = min(512, tokens_here)
    block_count = tokens_here // block_rows
    shape_blocks = (block_count, block_rows, heads_here, HEAD_DIM)
    active_q = activate(queries).reshape(shape_blocks)
    active_k = activate(keys).reshape(shape_blocks)
    active_v = activate(values).reshape(shape_blocks)
    block_states = jnp.einsum(
        "nshd,nshe->nhde", active_k, active_v, preferred_element_type=jnp.float32
    )
    span_total = jnp.sum(block_states, axis=0)
    earlier_local = jnp.cumsum(block_states, axis=0) - block_states
    causal_mask = jnp.tril(jnp.ones((block_rows, block_rows), jnp.float32))
    scores = jnp.einsum("nthd,nshd->nhts", active_q, active_k, preferred_element_type=jnp.float32)
    scores = (scores * causal_mask).astype(jnp.bfloat16)
    within_block = jnp.einsum(
        "nhts,nshd->nthd", scores, active_v, preferred_element_type=jnp.float32
    )
    within_rows = within_block.reshape(tokens_here, feature_count)
    prefix, within_rows = exclusive_prefix(span_total, "seq", within_rows)
    within_block, prefix = lax.optimization_barrier((within_block, prefix))
    before = (prefix[None] + earlier_local).astype(jnp.bfloat16)
    if block_count == 1:
        identity = jnp.eye(heads_here, dtype=jnp.bfloat16)
        diagonal = jnp.einsum("hde,hg->hdge", before[0], identity).reshape(
            feature_count, feature_count
        )
        from_state = jnp.dot(
            active_q.reshape(tokens_here, feature_count), diagonal,
            preferred_element_type=jnp.float32,
        )
    else:
        from_state = jnp.einsum(
            "nthd,nhde->nthe", active_q, before, preferred_element_type=jnp.float32
        ).reshape(tokens_here, feature_count)
    attended = within_rows + from_state
    square_sums = jnp.sum(attended * attended, axis=-1)
    gate = jax.nn.sigmoid(gate_logits.astype(jnp.float32))
    gated = (attended * gate).astype(jnp.bfloat16)
    total_squares = butterfly_sum(square_sums, "head")
    reduced = line_reduce_scatter(gated, out_weight, "head", total_squares)
    return reduced.astype(jnp.bfloat16)


def solution(mesh):
    return jax.shard_map(
        body,
        mesh=mesh,
        in_specs=(
            P("seq", "head"),
            P("seq", "head"),
            P("seq", "head"),
            P("seq", "head"),
            P("head", None),
        ),
        out_specs=P("seq", "head"),
        check_vma=False,
    )
```

```python
import jax
import jax.numpy as jnp
from jax import lax
from jax.sharding import PartitionSpec as P

HEADS = 32
HEAD_DIM = 128


def activate(raw_input):
    return jax.nn.silu(raw_input.astype(jnp.float32)).astype(jnp.bfloat16)


def exclusive_prefix(span_total, axis_name, companion):
    count = lax.axis_size(axis_name)
    my_index = lax.axis_index(axis_name)
    if count & (count - 1):
        shards = lax.all_gather(
            span_total[None].astype(jnp.bfloat16), axis_name, axis=0, tiled=True
        ).astype(jnp.float32)
        positions = jnp.arange(count, dtype=jnp.int32)
        weights = (positions < my_index).astype(jnp.float32)
        return jnp.sum(shards * weights[:, None, None, None], axis=0), companion
    group_total = span_total
    prefix = jnp.zeros_like(span_total)
    bit = 1
    while bit < count:
        if bit * 2 == count and bit > 1:
            group_total, companion = lax.optimization_barrier((group_total, companion))
        pairs = [(i, i ^ bit) for i in range(count)]
        arrived = lax.ppermute(group_total.astype(jnp.bfloat16), axis_name, pairs)
        arrived = arrived.astype(jnp.float32)
        upper = ((my_index // bit) % 2).astype(jnp.float32)
        prefix = prefix + upper * arrived
        group_total = group_total + arrived
        bit *= 2
    return prefix, companion


def shard_product(gated, out_weight, shard, width):
    columns = lax.dynamic_slice_in_dim(out_weight, shard * width, width, axis=1)
    return jnp.dot(gated, columns, preferred_element_type=jnp.float32)


def butterfly_sum(values, axis_name):
    count = lax.axis_size(axis_name)
    if count & (count - 1):
        return lax.psum(values, axis_name)
    bit = 1
    while bit < count:
        values = values + lax.ppermute(values, axis_name, [(i, i ^ bit) for i in range(count)])
        bit *= 2
    return values


def line_reduce_scatter(gated, out_weight, axis_name, square_sums):
    count = lax.axis_size(axis_name)
    here = lax.axis_index(axis_name)
    width = out_weight.shape[1] // count
    from_left = None
    from_right = None
    power_of_two = not count & (count - 1)
    if power_of_two:
        total_squares = square_sums + lax.ppermute(
            square_sums, axis_name, [(i, i ^ 1) for i in range(count)]
        )
    else:
        total_squares = lax.psum(square_sums, axis_name)
    for step in range(1, count):
        if power_of_two and step == 2:
            bit = 2
            while bit < count:
                total_squares = total_squares + lax.ppermute(
                    total_squares, axis_name, [(i, i ^ bit) for i in range(count)]
                )
                bit *= 2
        right_shard = jnp.clip(here + count - step, 0, count - 1)
        left_shard = jnp.clip(here - count + step, 0, count - 1)
        if 2 * step <= count:
            shard = jnp.where(here < step, right_shard, left_shard)
            product = shard_product(gated, out_weight, shard, width).astype(jnp.bfloat16)
            if step == 1:
                product, total_squares = lax.optimization_barrier((product, total_squares))
            else:
                product = lax.optimization_barrier(product)
            to_right = product.astype(jnp.float32)
            if from_left is not None:
                to_right = to_right + from_left + from_right
            to_right = to_right.astype(jnp.bfloat16)
            if step == 2:
                to_right, total_squares = lax.optimization_barrier((to_right, total_squares))
            to_left = to_right
        else:
            to_right = shard_product(gated, out_weight, right_shard, width).astype(jnp.bfloat16)
            to_left = shard_product(gated, out_weight, left_shard, width).astype(jnp.bfloat16)
            if step == 1:
                to_right, to_left, total_squares = lax.optimization_barrier(
                    (to_right, to_left, total_squares)
                )
            else:
                to_right, to_left = lax.optimization_barrier((to_right, to_left))
            if from_left is not None:
                to_right = (to_right.astype(jnp.float32) + from_left).astype(jnp.bfloat16)
                to_left = (to_left.astype(jnp.float32) + from_right).astype(jnp.bfloat16)
        right_pairs = [(i, i + 1) for i in range(step) if i + 1 < count]
        left_pairs = [(i, i - 1) for i in range(count - step, count) if i >= 1]
        from_left = lax.ppermute(to_right, axis_name, right_pairs).astype(jnp.float32)
        from_right = lax.ppermute(to_left, axis_name, left_pairs).astype(jnp.float32)
    own = shard_product(gated, out_weight, here, width).astype(jnp.bfloat16)
    own = own.astype(jnp.float32)
    scaling = lax.rsqrt(total_squares / (HEADS * HEAD_DIM) + 1e-06)
    if from_left is not None:
        own = own + from_left + from_right
    return own * scaling[:, None]


def body(queries, keys, values, gate_logits, out_weight):
    tokens_here = queries.shape[0]
    feature_count = queries.shape[1]
    heads_here = feature_count // HEAD_DIM
    block_rows = min(512, tokens_here)
    block_count = tokens_here // block_rows
    shape_blocks = (block_count, block_rows, heads_here, HEAD_DIM)
    active_q = activate(queries).reshape(shape_blocks)
    active_k = activate(keys).reshape(shape_blocks)
    active_v = activate(values).reshape(shape_blocks)
    block_states = jnp.einsum(
        "nshd,nshe->nhde", active_k, active_v, preferred_element_type=jnp.float32
    )
    span_total = jnp.sum(block_states, axis=0)
    earlier_local = jnp.cumsum(block_states, axis=0) - block_states
    causal_mask = jnp.tril(jnp.ones((block_rows, block_rows), jnp.float32))
    scores = jnp.einsum("nthd,nshd->nhts", active_q, active_k, preferred_element_type=jnp.float32)
    scores = (scores * causal_mask).astype(jnp.bfloat16)
    within_block = jnp.einsum(
        "nhts,nshd->nthd", scores, active_v, preferred_element_type=jnp.float32
    )
    within_rows = within_block.reshape(tokens_here, feature_count)
    prefix, within_rows = exclusive_prefix(span_total, "seq", within_rows)
    within_block, prefix = lax.optimization_barrier((within_block, prefix))
    before = (prefix[None] + earlier_local).astype(jnp.bfloat16)
    if block_count == 1:
        identity = jnp.eye(heads_here, dtype=jnp.bfloat16)
        diagonal = jnp.einsum("hde,hg->hdge", before[0], identity).reshape(
            feature_count, feature_count
        )
        from_state = jnp.dot(
            active_q.reshape(tokens_here, feature_count), diagonal,
            preferred_element_type=jnp.float32,
        )
    else:
        from_state = jnp.einsum(
            "nthd,nhde->nthe", active_q, before, preferred_element_type=jnp.float32
        ).reshape(tokens_here, feature_count)
    attended = within_rows + from_state
    square_sums = jnp.sum(attended * attended, axis=-1)
    gate = jax.nn.sigmoid(gate_logits.astype(jnp.float32))
    gated = (attended * gate).astype(jnp.bfloat16)
    reduced = line_reduce_scatter(gated, out_weight, "head", square_sums)
    return reduced.astype(jnp.bfloat16)


def solution(mesh):
    return jax.shard_map(
        body,
        mesh=mesh,
        in_specs=(
            P("seq", "head"),
            P("seq", "head"),
            P("seq", "head"),
            P("seq", "head"),
            P("head", None),
        ),
        out_specs=P("seq", "head"),
        check_vma=False,
    )
```

```python
import jax
import jax.numpy as jnp
from jax import lax
from jax.sharding import PartitionSpec as P

HEADS = 32
HEAD_DIM = 128


def activate(raw_input):
    return jax.nn.silu(raw_input.astype(jnp.float32)).astype(jnp.bfloat16)


def exclusive_prefix(span_total, axis_name, companion):
    count = lax.axis_size(axis_name)
    my_index = lax.axis_index(axis_name)
    if count & (count - 1):
        shards = lax.all_gather(
            span_total[None].astype(jnp.bfloat16), axis_name, axis=0, tiled=True
        ).astype(jnp.float32)
        positions = jnp.arange(count, dtype=jnp.int32)
        weights = (positions < my_index).astype(jnp.float32)
        return jnp.sum(shards * weights[:, None, None, None], axis=0), companion
    group_total = span_total
    prefix = jnp.zeros_like(span_total)
    bit = 1
    while bit < count:
        if bit * 2 == count and bit > 1:
            group_total, companion = lax.optimization_barrier((group_total, companion))
        pairs = [(i, i ^ bit) for i in range(count)]
        arrived = lax.ppermute(group_total.astype(jnp.bfloat16), axis_name, pairs)
        arrived = arrived.astype(jnp.float32)
        upper = ((my_index // bit) % 2).astype(jnp.float32)
        prefix = prefix + upper * arrived
        group_total = group_total + arrived
        bit *= 2
    return prefix, companion


def shard_product(gated, out_weight, shard, width):
    columns = lax.dynamic_slice_in_dim(out_weight, shard * width, width, axis=1)
    return jnp.dot(gated, columns, preferred_element_type=jnp.float32)


def butterfly_sum(values, axis_name):
    count = lax.axis_size(axis_name)
    if count & (count - 1):
        return lax.psum(values, axis_name)
    bit = 1
    while bit < count:
        values = values + lax.ppermute(values, axis_name, [(i, i ^ bit) for i in range(count)])
        bit *= 2
    return values


def line_reduce_scatter(gated, out_weight, axis_name, square_sums):
    count = lax.axis_size(axis_name)
    here = lax.axis_index(axis_name)
    width = out_weight.shape[1] // count
    from_left = None
    from_right = None
    power_of_two = not count & (count - 1)
    if power_of_two:
        total_squares = square_sums + lax.ppermute(
            square_sums, axis_name, [(i, i ^ 1) for i in range(count)]
        )
    else:
        total_squares = lax.psum(square_sums, axis_name)
    for step in range(1, count):
        if power_of_two and step == 2:
            bit = 2
            while bit < count:
                total_squares = total_squares + lax.ppermute(
                    total_squares, axis_name, [(i, i ^ bit) for i in range(count)]
                )
                bit *= 2
        right_shard = jnp.clip(here + count - step, 0, count - 1)
        left_shard = jnp.clip(here - count + step, 0, count - 1)
        if 2 * step <= count:
            shard = jnp.where(here < step, right_shard, left_shard)
            product = shard_product(gated, out_weight, shard, width).astype(jnp.bfloat16)
            if step == 1:
                product, total_squares = lax.optimization_barrier((product, total_squares))
            else:
                product = lax.optimization_barrier(product)
            to_right = product.astype(jnp.float32)
            if from_left is not None:
                to_right = to_right + from_left + from_right
            to_right = to_right.astype(jnp.bfloat16)
            if step == 2:
                to_right, total_squares = lax.optimization_barrier((to_right, total_squares))
            to_left = to_right
        else:
            to_right = shard_product(gated, out_weight, right_shard, width).astype(jnp.bfloat16)
            to_left = shard_product(gated, out_weight, left_shard, width).astype(jnp.bfloat16)
            if step == 1:
                to_right, to_left, total_squares = lax.optimization_barrier(
                    (to_right, to_left, total_squares)
                )
            else:
                to_right, to_left = lax.optimization_barrier((to_right, to_left))
            if from_left is not None:
                to_right = (to_right.astype(jnp.float32) + from_left).astype(jnp.bfloat16)
                to_left = (to_left.astype(jnp.float32) + from_right).astype(jnp.bfloat16)
        right_pairs = [(i, i + 1) for i in range(step) if i + 1 < count]
        left_pairs = [(i, i - 1) for i in range(count - step, count) if i >= 1]
        from_left = sum(
            lax.ppermute(to_right, axis_name, [pair]).astype(jnp.float32) for pair in right_pairs
        )
        from_right = sum(
            lax.ppermute(to_left, axis_name, [pair]).astype(jnp.float32) for pair in left_pairs
        )
    own = shard_product(gated, out_weight, here, width).astype(jnp.bfloat16)
    own = own.astype(jnp.float32)
    scaling = lax.rsqrt(total_squares / (HEADS * HEAD_DIM) + 1e-06)
    if from_left is not None:
        own = own + from_left + from_right
    return own * scaling[:, None]


def body(queries, keys, values, gate_logits, out_weight):
    tokens_here = queries.shape[0]
    feature_count = queries.shape[1]
    heads_here = feature_count // HEAD_DIM
    block_rows = min(512, tokens_here)
    block_count = tokens_here // block_rows
    shape_blocks = (block_count, block_rows, heads_here, HEAD_DIM)
    active_q = activate(queries).reshape(shape_blocks)
    active_k = activate(keys).reshape(shape_blocks)
    active_v = activate(values).reshape(shape_blocks)
    block_states = jnp.einsum(
        "nshd,nshe->nhde", active_k, active_v, preferred_element_type=jnp.float32
    )
    span_total = jnp.sum(block_states, axis=0)
    earlier_local = jnp.cumsum(block_states, axis=0) - block_states
    causal_mask = jnp.tril(jnp.ones((block_rows, block_rows), jnp.float32))
    scores = jnp.einsum("nthd,nshd->nhts", active_q, active_k, preferred_element_type=jnp.float32)
    scores = (scores * causal_mask).astype(jnp.bfloat16)
    within_block = jnp.einsum(
        "nhts,nshd->nthd", scores, active_v, preferred_element_type=jnp.float32
    )
    within_rows = within_block.reshape(tokens_here, feature_count)
    prefix, within_rows = exclusive_prefix(span_total, "seq", within_rows)
    within_block, prefix = lax.optimization_barrier((within_block, prefix))
    before = (prefix[None] + earlier_local).astype(jnp.bfloat16)
    if block_count == 1:
        identity = jnp.eye(heads_here, dtype=jnp.bfloat16)
        diagonal = jnp.einsum("hde,hg->hdge", before[0], identity).reshape(
            feature_count, feature_count
        )
        from_state = jnp.dot(
            active_q.reshape(tokens_here, feature_count), diagonal,
            preferred_element_type=jnp.float32,
        )
    else:
        from_state = jnp.einsum(
            "nthd,nhde->nthe", active_q, before, preferred_element_type=jnp.float32
        ).reshape(tokens_here, feature_count)
    attended = within_rows + from_state
    square_sums = jnp.sum(attended * attended, axis=-1)
    gate = jax.nn.sigmoid(gate_logits.astype(jnp.float32))
    gated = (attended * gate).astype(jnp.bfloat16)
    reduced = line_reduce_scatter(gated, out_weight, "head", square_sums)
    return reduced.astype(jnp.bfloat16)


def solution(mesh):
    return jax.shard_map(
        body,
        mesh=mesh,
        in_specs=(
            P("seq", "head"),
            P("seq", "head"),
            P("seq", "head"),
            P("seq", "head"),
            P("head", None),
        ),
        out_specs=P("seq", "head"),
        check_vma=False,
    )
```

```python
import jax
import jax.numpy as jnp
from jax import lax
from jax.sharding import PartitionSpec as P

HEADS = 32
HEAD_DIM = 128


def activate(raw_input):
    return jax.nn.silu(raw_input.astype(jnp.float32)).astype(jnp.bfloat16)


def exclusive_prefix(span_total, axis_name, companion):
    count = lax.axis_size(axis_name)
    my_index = lax.axis_index(axis_name)
    if count & (count - 1):
        shards = lax.all_gather(
            span_total[None].astype(jnp.bfloat16), axis_name, axis=0, tiled=True
        ).astype(jnp.float32)
        positions = jnp.arange(count, dtype=jnp.int32)
        weights = (positions < my_index).astype(jnp.float32)
        return jnp.sum(shards * weights[:, None, None, None], axis=0), companion
    group_total = span_total
    prefix = jnp.zeros_like(span_total)
    bit = 1
    while bit < count:
        if bit * 2 == count and bit > 1:
            group_total, companion = lax.optimization_barrier((group_total, companion))
        pairs = [(i, i ^ bit) for i in range(count)]
        arrived = lax.ppermute(group_total.astype(jnp.bfloat16), axis_name, pairs)
        arrived = arrived.astype(jnp.float32)
        upper = ((my_index // bit) % 2).astype(jnp.float32)
        prefix = prefix + upper * arrived
        group_total = group_total + arrived
        bit *= 2
    return prefix, companion


def shard_product(gated, out_weight, shard, width):
    columns = lax.dynamic_slice_in_dim(out_weight, shard * width, width, axis=1)
    return jnp.dot(gated, columns, preferred_element_type=jnp.float32)


def butterfly_sum(values, axis_name):
    count = lax.axis_size(axis_name)
    if count & (count - 1):
        return lax.psum(values, axis_name)
    bit = 1
    while bit < count:
        values = values + lax.ppermute(values, axis_name, [(i, i ^ bit) for i in range(count)])
        bit *= 2
    return values


def line_reduce_scatter(gated, out_weight, axis_name, square_sums):
    count = lax.axis_size(axis_name)
    here = lax.axis_index(axis_name)
    width = out_weight.shape[1] // count
    tokens = gated.shape[0]
    extra = 8 * (-(-tokens // (8 * width)))

    def packed(main, squares):
        flat = jnp.zeros((extra * width,), jnp.float32).at[:tokens].set(squares)
        rows = flat.reshape(extra, width).astype(jnp.bfloat16)
        return jnp.concatenate([main.astype(jnp.bfloat16), rows], axis=0)

    def unpacked(block):
        block = block.astype(jnp.float32)
        return block[:tokens], block[tokens:].reshape(-1)[:tokens]

    from_left = None
    from_right = None
    left_squares = jnp.zeros_like(square_sums)
    right_squares = jnp.zeros_like(square_sums)
    for step in range(1, count):
        right_shard = jnp.clip(here + count - step, 0, count - 1)
        left_shard = jnp.clip(here - count + step, 0, count - 1)
        if 2 * step <= count:
            shard = jnp.where(here < step, right_shard, left_shard)
            product = shard_product(gated, out_weight, shard, width).astype(jnp.bfloat16)
            product = lax.optimization_barrier(product)
            main = product.astype(jnp.float32)
            if from_left is not None:
                main = main + from_left + from_right
            to_right = packed(main, square_sums + left_squares + right_squares)
            to_left = to_right
        else:
            product_r = shard_product(gated, out_weight, right_shard, width).astype(jnp.bfloat16)
            product_l = shard_product(gated, out_weight, left_shard, width).astype(jnp.bfloat16)
            product_r, product_l = lax.optimization_barrier((product_r, product_l))
            to_right = packed(product_r.astype(jnp.float32) + from_left, square_sums + left_squares)
            to_left = packed(product_l.astype(jnp.float32) + from_right, square_sums + right_squares)
        right_pairs = [(i, i + 1) for i in range(step) if i + 1 < count]
        left_pairs = [(i, i - 1) for i in range(count - step, count) if i >= 1]
        from_left, left_squares = unpacked(lax.ppermute(to_right, axis_name, right_pairs))
        from_right, right_squares = unpacked(lax.ppermute(to_left, axis_name, left_pairs))
    own = shard_product(gated, out_weight, here, width).astype(jnp.bfloat16)
    own = own.astype(jnp.float32)
    total_squares = square_sums + left_squares + right_squares
    scaling = lax.rsqrt(total_squares / (HEADS * HEAD_DIM) + 1e-06)
    if from_left is not None:
        own = own + from_left + from_right
    return own * scaling[:, None]


def body(queries, keys, values, gate_logits, out_weight):
    tokens_here = queries.shape[0]
    feature_count = queries.shape[1]
    heads_here = feature_count // HEAD_DIM
    block_rows = min(512, tokens_here)
    block_count = tokens_here // block_rows
    shape_blocks = (block_count, block_rows, heads_here, HEAD_DIM)
    active_q = activate(queries).reshape(shape_blocks)
    active_k = activate(keys).reshape(shape_blocks)
    active_v = activate(values).reshape(shape_blocks)
    block_states = jnp.einsum(
        "nshd,nshe->nhde", active_k, active_v, preferred_element_type=jnp.float32
    )
    span_total = jnp.sum(block_states, axis=0)
    earlier_local = jnp.cumsum(block_states, axis=0) - block_states
    causal_mask = jnp.tril(jnp.ones((block_rows, block_rows), jnp.float32))
    scores = jnp.einsum("nthd,nshd->nhts", active_q, active_k, preferred_element_type=jnp.float32)
    scores = (scores * causal_mask).astype(jnp.bfloat16)
    within_block = jnp.einsum(
        "nhts,nshd->nthd", scores, active_v, preferred_element_type=jnp.float32
    )
    within_rows = within_block.reshape(tokens_here, feature_count)
    prefix, within_rows = exclusive_prefix(span_total, "seq", within_rows)
    within_block, prefix = lax.optimization_barrier((within_block, prefix))
    before = (prefix[None] + earlier_local).astype(jnp.bfloat16)
    if block_count == 1:
        identity = jnp.eye(heads_here, dtype=jnp.bfloat16)
        diagonal = jnp.einsum("hde,hg->hdge", before[0], identity).reshape(
            feature_count, feature_count
        )
        from_state = jnp.dot(
            active_q.reshape(tokens_here, feature_count), diagonal,
            preferred_element_type=jnp.float32,
        )
    else:
        from_state = jnp.einsum(
            "nthd,nhde->nthe", active_q, before, preferred_element_type=jnp.float32
        ).reshape(tokens_here, feature_count)
    attended = within_rows + from_state
    square_sums = jnp.sum(attended * attended, axis=-1)
    gate = jax.nn.sigmoid(gate_logits.astype(jnp.float32))
    gated = (attended * gate).astype(jnp.bfloat16)
    reduced = line_reduce_scatter(gated, out_weight, "head", square_sums)
    return reduced.astype(jnp.bfloat16)


def solution(mesh):
    return jax.shard_map(
        body,
        mesh=mesh,
        in_specs=(
            P("seq", "head"),
            P("seq", "head"),
            P("seq", "head"),
            P("seq", "head"),
            P("head", None),
        ),
        out_specs=P("seq", "head"),
        check_vma=False,
    )
```

```python
import jax
import jax.numpy as jnp
from jax import lax
from jax.sharding import PartitionSpec as P

HEADS = 32
HEAD_DIM = 128


def activate(raw_input):
    return jax.nn.silu(raw_input.astype(jnp.float32)).astype(jnp.bfloat16)


def exclusive_prefix(span_total, axis_name, companion):
    count = lax.axis_size(axis_name)
    my_index = lax.axis_index(axis_name)
    if count & (count - 1):
        shards = lax.all_gather(
            span_total[None].astype(jnp.bfloat16), axis_name, axis=0, tiled=True
        ).astype(jnp.float32)
        positions = jnp.arange(count, dtype=jnp.int32)
        weights = (positions < my_index).astype(jnp.float32)
        return jnp.sum(shards * weights[:, None, None, None], axis=0), companion
    group_total = span_total
    prefix = jnp.zeros_like(span_total)
    bit = 1
    while bit < count:
        if bit * 2 == count and bit > 1:
            group_total, companion = lax.optimization_barrier((group_total, companion))
        pairs = [(i, i ^ bit) for i in range(count)]
        arrived = lax.ppermute(group_total.astype(jnp.bfloat16), axis_name, pairs)
        arrived = arrived.astype(jnp.float32)
        upper = ((my_index // bit) % 2).astype(jnp.float32)
        prefix = prefix + upper * arrived
        group_total = group_total + arrived
        bit *= 2
    return prefix, companion


def shard_product(gated, out_weight, shard, width):
    columns = lax.dynamic_slice_in_dim(out_weight, shard * width, width, axis=1)
    return jnp.dot(gated, columns, preferred_element_type=jnp.float32)


def butterfly_sum(values, axis_name):
    count = lax.axis_size(axis_name)
    if count & (count - 1):
        return lax.psum(values, axis_name)
    bit = 1
    while bit < count:
        values = values + lax.ppermute(values, axis_name, [(i, i ^ bit) for i in range(count)])
        bit *= 2
    return values


def line_reduce_scatter(gated, out_weight, axis_name, square_sums):
    count = lax.axis_size(axis_name)
    here = lax.axis_index(axis_name)
    width = out_weight.shape[1] // count
    from_left = None
    from_right = None
    power_of_two = not count & (count - 1)
    if power_of_two:
        total_squares = square_sums + lax.ppermute(
            square_sums, axis_name, [(i, i ^ 1) for i in range(count)]
        )
    else:
        total_squares = lax.psum(square_sums, axis_name)
    for step in range(1, count):
        if power_of_two and step == 2:
            bit = 2
            while bit < count:
                total_squares = total_squares + lax.ppermute(
                    total_squares, axis_name, [(i, i ^ bit) for i in range(count)]
                )
                bit *= 2
        right_shard = jnp.clip(here + count - step, 0, count - 1)
        left_shard = jnp.clip(here - count + step, 0, count - 1)
        if 2 * step <= count:
            shard = jnp.where(here < step, right_shard, left_shard)
            product = shard_product(gated, out_weight, shard, width).astype(jnp.bfloat16)
            if step == 1:
                product, total_squares = lax.optimization_barrier((product, total_squares))
            else:
                product = lax.optimization_barrier(product)
            to_right = product.astype(jnp.float32)
            if from_left is not None:
                to_right = to_right + from_left + from_right
            to_right = to_right.astype(jnp.bfloat16)
            if step == 2:
                to_right, total_squares = lax.optimization_barrier((to_right, total_squares))
            to_left = to_right
        else:
            to_right = shard_product(gated, out_weight, right_shard, width).astype(jnp.bfloat16)
            to_left = shard_product(gated, out_weight, left_shard, width).astype(jnp.bfloat16)
            if step == 1:
                to_right, to_left, total_squares = lax.optimization_barrier(
                    (to_right, to_left, total_squares)
                )
            else:
                to_right, to_left = lax.optimization_barrier((to_right, to_left))
            if from_left is not None:
                to_right = (to_right.astype(jnp.float32) + from_left).astype(jnp.bfloat16)
                to_left = (to_left.astype(jnp.float32) + from_right).astype(jnp.bfloat16)
        right_pairs = [(i, i + 1) for i in range(step) if i + 1 < count]
        left_pairs = [(i, i - 1) for i in range(count - step, count) if i >= 1]
        from_left = lax.ppermute(to_right, axis_name, right_pairs).astype(jnp.float32)
        from_right = lax.ppermute(to_left, axis_name, left_pairs).astype(jnp.float32)
    own = shard_product(gated, out_weight, here, width).astype(jnp.bfloat16)
    own = own.astype(jnp.float32)
    scaling = lax.rsqrt(total_squares / (HEADS * HEAD_DIM) + 1e-06)
    if from_left is not None:
        own = own + from_left + from_right
    return own * scaling[:, None]


def body(queries, keys, values, gate_logits, out_weight):
    tokens_here = queries.shape[0]
    feature_count = queries.shape[1]
    heads_here = feature_count // HEAD_DIM
    block_rows = min(512, tokens_here)
    block_count = tokens_here // block_rows
    shape_blocks = (block_count, block_rows, heads_here, HEAD_DIM)
    active_q = activate(queries).reshape(shape_blocks)
    active_k = activate(keys).reshape(shape_blocks)
    active_v = activate(values).reshape(shape_blocks)
    block_states = jnp.einsum(
        "nshd,nshe->nhde", active_k, active_v, preferred_element_type=jnp.float32
    )
    span_total = jnp.sum(block_states, axis=0)
    earlier_local = jnp.cumsum(block_states, axis=0) - block_states
    causal_mask = jnp.tril(jnp.ones((block_rows, block_rows), jnp.float32))
    scores = jnp.einsum("nthd,nshd->nhts", active_q, active_k, preferred_element_type=jnp.float32)
    scores = (scores * causal_mask).astype(jnp.bfloat16)
    within_block = jnp.einsum(
        "nhts,nshd->nthd", scores, active_v, preferred_element_type=jnp.float32
    )
    within_rows = within_block.reshape(tokens_here, feature_count)
    prefix, within_rows = exclusive_prefix(span_total, "seq", within_rows)
    before = (prefix[None] + earlier_local).astype(jnp.bfloat16)
    if block_count == 1:
        identity = jnp.eye(heads_here, dtype=jnp.bfloat16)
        diagonal = jnp.einsum("hde,hg->hdge", before[0], identity).reshape(
            feature_count, feature_count
        )
        from_state = jnp.dot(
            active_q.reshape(tokens_here, feature_count), diagonal,
            preferred_element_type=jnp.float32,
        )
    else:
        from_state = jnp.einsum(
            "nthd,nhde->nthe", active_q, before, preferred_element_type=jnp.float32
        ).reshape(tokens_here, feature_count)
    attended = within_rows + from_state
    square_sums = jnp.sum(attended * attended, axis=-1)
    gate = jax.nn.sigmoid(gate_logits.astype(jnp.float32))
    gated = (attended * gate).astype(jnp.bfloat16)
    reduced = line_reduce_scatter(gated, out_weight, "head", square_sums)
    return reduced.astype(jnp.bfloat16)


def solution(mesh):
    return jax.shard_map(
        body,
        mesh=mesh,
        in_specs=(
            P("seq", "head"),
            P("seq", "head"),
            P("seq", "head"),
            P("seq", "head"),
            P("head", None),
        ),
        out_specs=P("seq", "head"),
        check_vma=False,
    )
```
